32 devices in a mesh: groups: 2 (over y), tensor: 4 (over x, core), dp: 4 (over z).
Axes of the slice: x: 2, y: 2, z: 4, core: 2. Of those that a mesh axis runs over, the one named last changes fastest.
Arguments:
- tokens: bfloat16 [65536, 4096], P(('groups', 'dp'), 'tensor'), parts along dimension 0, may hold values from -6 to 6
- cotangent: bfloat16 [65536, 4096], P(('groups', 'dp'), 'tensor'), parts along dimension 0, may hold values from -6 to 6
- w_first: bfloat16 [16, 256, 256], P('tensor'), may hold values from -0.375 to 0.375
- w_second: bfloat16 [16, 256, 256], P('tensor'), may hold values from -0.375 to 0.375
Outputs:
- grad_tokens: bfloat16 [65536, 4096], P(('groups', 'dp'), 'tensor'), parts along dimension 0
- grad_first: float32 [32, 256, 256], P(('groups', 'tensor'), 'dp'), parts along dimension 0
- grad_second: float32 [32, 256, 256], P(('groups', 'tensor'), 'dp'), parts along dimension 0
The draws below stay inside these ranges and needn't reach their ends.
There are 2 independent parts, one for each index of `groups`. The reference program is written for one: setup_inputs(seed, part) draws one part's arguments, and reference() takes and returns one part's arrays. A program takes and returns all parts, laid end to end along the dimension named above; an argument that names none is the same for every part. Nothing has to cross between parts.
All inputs are finite; a program needn't handle non-finite values.
Results may differ from the reference program's by a relative error of at most 0.0065.
Values may be sent and summed in bfloat16 or wider, within the bound.
No kernel may reach another device: no remote copies, remote signals or barrier semaphores. Data moves between devices by JAX's collectives and lax.ppermute only.
A program may use at most 192 MiB of HBM per device.

```python
import math
import jax
import jax.numpy as jnp

NB = 16
BS = 256
TOKENS = 32768
D = 4096


def levels(key, extent, split, low, high):
    level, own = 1.0, jax.random.fold_in(key, 6)
    for axis_at, parts in split:
        draws = jnp.exp(jax.random.uniform(jax.random.fold_in(own, axis_at), (parts,), jnp.float32, low / len(split), high / len(split)))
        level = level * jnp.repeat(draws, extent[axis_at] // parts).reshape([-1 if axis == axis_at else 1 for axis in range(len(extent))])
    return level


def normal_values(stream_key, shape, deviation, most, cuts=(), held_as=jnp.bfloat16):
    loudness = levels(stream_key, shape, cuts, -0.22, 0.18) if cuts else 1.0
    entries = jax.random.normal(stream_key, shape, jnp.float32) * deviation * loudness
    return jnp.minimum(jnp.maximum(entries, -most), most).astype(held_as)


def setup_inputs(seed: int = 0, part: int = 0) -> dict:
    splits = jax.random.split(jax.random.key(seed), 5)
    part_splits = jax.random.split(jax.random.fold_in(splits[4], part), 5)
    return {
        "tokens": normal_values(part_splits[0], (TOKENS, D), 1.0, 6.0, ((0, 4), (1, 4))),
        "cotangent": normal_values(part_splits[1], (TOKENS, D), 1.0, 6.0, ((0, 4), (1, 4))),
        "w_first": normal_values(splits[2], (NB, BS, BS), BS ** -0.5, 0.375, ((0, 4),)),
        "w_second": normal_values(splits[3], (NB, BS, BS), BS ** -0.5, 0.375, ((0, 4),)),
    }


def reference(tokens, cotangent, w_first, w_second):
    sub_width = BS // NB
    inputs = tokens.reshape(TOKENS, NB, BS).astype(jnp.float32)
    upstream = cotangent.reshape(TOKENS, NB, BS).astype(jnp.float32)
    hidden = jnp.einsum('tbi,bij->tbj', inputs, w_first.astype(jnp.float32)).astype(jnp.bfloat16)
    permuted = hidden.reshape(TOKENS, NB, NB, sub_width).transpose(0, 2, 3, 1).reshape(TOKENS, NB, BS)
    active = jnp.maximum(permuted, jnp.zeros((), jnp.bfloat16))
    grad_scale = 1.0 / math.sqrt(TOKENS)
    grad_second = jnp.einsum('tck,tco->cko', active.astype(jnp.float32), upstream) * grad_scale
    backed = jnp.einsum('tco,cko->tck', upstream, w_second.astype(jnp.float32))
    masked = jnp.where(permuted > 0, backed, jnp.zeros((), jnp.float32)).astype(jnp.bfloat16)
    unmixed = masked.reshape(TOKENS, NB, sub_width, NB).transpose(0, 3, 1, 2).reshape(TOKENS, NB, BS)
    unmixed_wide = unmixed.astype(jnp.float32)
    grad_first = jnp.einsum('tbi,tbj->bij', inputs, unmixed_wide) * grad_scale
    grad_tokens = jnp.einsum('tbj,bij->tbi', unmixed_wide, w_first.astype(jnp.float32)).astype(jnp.bfloat16)
    return (grad_tokens.reshape(TOKENS, NB * BS), grad_first, grad_second)
```

```python
import math

import jax
import jax.numpy as jnp
from jax import lax
from jax.sharding import PartitionSpec as P

NB = 16
CHUNKS = 4


def expanded_weights(w_first, w_second, n_dev):
    blk_local, bs, _ = w_first.shape
    sub = bs // NB
    eye = jnp.eye(blk_local, dtype=jnp.bool_)
    zero = jnp.zeros((), w_first.dtype)
    w1r = w_first.reshape(blk_local, bs, n_dev, blk_local, sub)
    w1p = jnp.where(
        eye[:, None, None, None, :, None], w1r[:, :, :, :, None, :], zero
    ).reshape(blk_local * bs, blk_local * bs)
    w2r = w_second.reshape(blk_local, sub, n_dev, blk_local, bs).transpose(0, 4, 2, 3, 1)
    w2p = jnp.where(
        eye[:, None, None, :, None, None], w2r[:, :, :, None, :, :], zero
    ).reshape(blk_local * bs, blk_local * bs)
    w1t = w_first.reshape(blk_local, bs, NB, sub).transpose(2, 3, 0, 1)
    w1tp = jnp.where(
        eye[None, :, None, :, None], w1t[:, None, :, :, :], zero
    ).reshape(blk_local * bs, blk_local * bs)
    return w1p, w2p, w1tp


def shards(tokens, cotangent, w_first, w_second):
    tok_rows = tokens.shape[0]
    blk_local, bs, _ = w_first.shape
    feat = blk_local * bs
    sub = bs // NB
    n_dev = lax.axis_size("tensor")
    dp_count = lax.axis_size("dp")
    grad_scale = 1.0 / math.sqrt(tok_rows * dp_count)
    w1p, w2p, w1tp = expanded_weights(w_first, w_second, n_dev)
    step = tok_rows // CHUNKS

    gf_acc = None
    gs_acc = None
    outs = []
    for k in range(CHUNKS):
        x = tokens[k * step:(k + 1) * step]
        cot = cotangent[k * step:(k + 1) * step]
        hidden = jnp.dot(x, w1p, preferred_element_type=jnp.float32).astype(jnp.bfloat16)
        moved = lax.all_to_all(
            hidden.reshape(step, n_dev, feat // n_dev), "tensor", 1, 1, tiled=True
        ).reshape(step, feat)
        active = jnp.maximum(moved, jnp.zeros((), jnp.bfloat16))
        gs = lax.dot_general(
            active, cot, (((0,), (0,)), ((), ())), preferred_element_type=jnp.float32
        )
        backed = jnp.dot(cot, w2p, preferred_element_type=jnp.float32)
        masked = jnp.where(moved > 0, backed, 0.0).astype(jnp.bfloat16)
        returned = lax.all_to_all(
            masked.reshape(step, n_dev, feat // n_dev), "tensor", 1, 1, tiled=True
        ).reshape(step, feat)
        gt = jnp.dot(returned, w1tp, preferred_element_type=jnp.float32).astype(jnp.bfloat16)
        outs.append(gt)
        gf = lax.dot_general(
            x, returned, (((0,), (0,)), ((), ())), preferred_element_type=jnp.float32
        )
        gf_acc = gf if gf_acc is None else gf_acc + gf
        gs_acc = gs if gs_acc is None else gs_acc + gs

    grad_tokens = jnp.concatenate(outs, axis=0)
    gf5 = gf_acc.reshape(blk_local, bs, NB, blk_local, sub)
    first_term = jnp.diagonal(gf5, axis1=0, axis2=3).transpose(3, 0, 1, 2)
    first_term = first_term.reshape(blk_local, bs, bs) * grad_scale
    gs6 = gs_acc.reshape(n_dev, blk_local, blk_local, sub, blk_local, bs)
    gsd = jnp.diagonal(gs6, axis1=1, axis2=4)
    second_term = gsd.transpose(4, 2, 0, 1, 3).reshape(blk_local, bs, bs) * grad_scale
    grad_first, grad_second = (
        lax.psum_scatter(first_term, "dp", scatter_dimension=1, tiled=True),
        lax.psum_scatter(second_term, "dp", scatter_dimension=1, tiled=True),
    )
    return (grad_tokens, grad_first, grad_second)


def solution(mesh):
    return jax.shard_map(
        shards,
        mesh=mesh,
        in_specs=(
            P(("groups", "dp"), "tensor"),
            P(("groups", "dp"), "tensor"),
            P("tensor", None, None),
            P("tensor", None, None),
        ),
        out_specs=(
            P(("groups", "dp"), "tensor"),
            P(("groups", "tensor"), "dp", None),
            P(("groups", "tensor"), "dp", None),
        ),
        check_vma=False,
    )
```

```python
import math

import jax
import jax.numpy as jnp
from jax import lax
from jax.sharding import PartitionSpec as P

NB = 16
CHUNKS = 4


def expanded_weights(w_first, w_second, n_dev, order):
    blk_local, bs, _ = w_first.shape
    sub = bs // NB
    feat = blk_local * bs
    eye = jnp.eye(blk_local, dtype=jnp.bool_)
    zero = jnp.zeros((), w_first.dtype)
    w1r = jnp.take(w_first.reshape(blk_local, bs, n_dev, blk_local, sub), order, axis=2)
    w1p = jnp.where(
        eye[:, None, None, None, :, None], w1r[:, :, :, :, None, :], zero
    ).reshape(feat, feat)
    w2r = jnp.take(w_second.reshape(blk_local, sub, n_dev, blk_local, bs), order, axis=2)
    w2r = w2r.transpose(0, 4, 2, 3, 1)
    w2p = jnp.where(
        eye[:, None, None, :, None, None], w2r[:, :, :, None, :, :], zero
    ).reshape(feat, feat)
    w1t = w1r.transpose(2, 3, 4, 0, 1)
    w1tp = jnp.where(
        eye[None, None, :, None, :, None], w1t[:, :, None, :, :, :], zero
    ).reshape(feat, feat)
    return w1p, w2p, w1tp


def exchange(pieces, n_dev):
    outs = [pieces[0]]
    for m in range(1, n_dev):
        outs.append(lax.ppermute(pieces[m], "tensor", [(i, i ^ m) for i in range(n_dev)]))
    return outs


def shards(tokens, cotangent, w_first, w_second):
    tok_rows = tokens.shape[0]
    blk_local, bs, _ = w_first.shape
    feat = blk_local * bs
    sub = bs // NB
    part = feat // lax.axis_size("tensor")
    n_dev = lax.axis_size("tensor")
    dp_count = lax.axis_size("dp")
    grad_scale = 1.0 / math.sqrt(tok_rows * dp_count)
    idx = lax.axis_index("tensor")
    order = jnp.bitwise_xor(idx, jnp.arange(n_dev, dtype=idx.dtype))
    w1p, w2p, w1tp = expanded_weights(w_first, w_second, n_dev, order)
    step = tok_rows // CHUNKS

    gf_acc = None
    gs_acc = None
    outs = []
    for k in range(CHUNKS):
        x = tokens[k * step:(k + 1) * step]
        cot = cotangent[k * step:(k + 1) * step]
        hidden = jnp.dot(x, w1p, preferred_element_type=jnp.float32).astype(jnp.bfloat16)
        backed = jnp.dot(cot, w2p, preferred_element_type=jnp.float32)
        moved = exchange([hidden[:, m * part:(m + 1) * part] for m in range(n_dev)], n_dev)
        masked = [
            jnp.where(moved[m] > 0, backed[:, m * part:(m + 1) * part], 0.0).astype(jnp.bfloat16)
            for m in range(n_dev)
        ]
        active = jnp.maximum(jnp.concatenate(moved, axis=1), jnp.zeros((), jnp.bfloat16))
        gs = lax.dot_general(
            active, cot, (((0,), (0,)), ((), ())), preferred_element_type=jnp.float32
        )
        returned = jnp.concatenate(exchange(masked, n_dev), axis=1)
        gt = jnp.dot(returned, w1tp, preferred_element_type=jnp.float32).astype(jnp.bfloat16)
        outs.append(gt)
        gf = lax.dot_general(
            x, returned, (((0,), (0,)), ((), ())), preferred_element_type=jnp.float32
        )
        gf_acc = gf if gf_acc is None else gf_acc + gf
        gs_acc = gs if gs_acc is None else gs_acc + gs

    grad_tokens = jnp.concatenate(outs, axis=0)
    gs6 = gs_acc.reshape(n_dev, blk_local, blk_local, sub, blk_local, bs)
    gsd = jnp.take(jnp.diagonal(gs6, axis1=1, axis2=4), order, axis=0)
    second_term = gsd.transpose(2, 0, 1, 4, 3).reshape(bs, blk_local, bs) * grad_scale
    grad_second = lax.psum_scatter(second_term, "dp", scatter_dimension=0, tiled=True)
    gf_acc, grad_second = lax.optimization_barrier((gf_acc, grad_second))
    gf6 = gf_acc.reshape(blk_local, bs, n_dev, blk_local, blk_local, sub)
    gfd = jnp.take(jnp.diagonal(gf6, axis1=0, axis2=4), order, axis=1)
    first_term = gfd.transpose(0, 4, 1, 2, 3).reshape(bs, blk_local, bs) * grad_scale
    grad_first = lax.psum_scatter(first_term, "dp", scatter_dimension=0, tiled=True)
    return (grad_tokens, grad_first.transpose(1, 0, 2), grad_second.transpose(1, 0, 2))


def solution(mesh):
    return jax.shard_map(
        shards,
        mesh=mesh,
        in_specs=(
            P(("groups", "dp"), "tensor"),
            P(("groups", "dp"), "tensor"),
            P("tensor", None, None),
            P("tensor", None, None),
        ),
        out_specs=(
            P(("groups", "dp"), "tensor"),
            P(("groups", "tensor"), "dp", None),
            P(("groups", "tensor"), "dp", None),
        ),
        check_vma=False,
    )
```

```python
import math

import jax
import jax.numpy as jnp
from jax import lax
from jax.sharding import PartitionSpec as P

NB = 16
CHUNKS = 4


def expanded_weights(w_first, w_second, n_dev, order):
    blk_local, bs, _ = w_first.shape
    sub = bs // NB
    feat = blk_local * bs
    eye = jnp.eye(blk_local, dtype=jnp.bool_)
    zero = jnp.zeros((), w_first.dtype)
    w1r = jnp.take(w_first.reshape(blk_local, bs, n_dev, blk_local, sub), order, axis=2)
    w1p = jnp.where(
        eye[:, None, None, None, :, None], w1r[:, :, :, :, None, :], zero
    ).reshape(feat, feat)
    w2r = jnp.take(w_second.reshape(blk_local, sub, n_dev, blk_local, bs), order, axis=2)
    w2r = w2r.transpose(0, 4, 2, 3, 1)
    w2p = jnp.where(
        eye[:, None, None, :, None, None], w2r[:, :, :, None, :, :], zero
    ).reshape(feat, feat)
    w1t = w1r.transpose(2, 3, 4, 0, 1)
    w1tp = jnp.where(
        eye[None, None, :, None, :, None], w1t[:, :, None, :, :, :], zero
    ).reshape(feat, feat)
    return w1p, w2p, w1tp


def exchange(pieces, n_dev):
    outs = [pieces[0]]
    for m in range(1, n_dev):
        outs.append(lax.ppermute(pieces[m], "tensor", [(i, i ^ m) for i in range(n_dev)]))
    return outs


def shards(tokens, cotangent, w_first, w_second):
    tok_rows = tokens.shape[0]
    blk_local, bs, _ = w_first.shape
    feat = blk_local * bs
    sub = bs // NB
    n_dev = lax.axis_size("tensor")
    part = feat // n_dev
    dp_count = lax.axis_size("dp")
    grad_scale = 1.0 / math.sqrt(tok_rows * dp_count)
    idx = lax.axis_index("tensor")
    order = jnp.bitwise_xor(idx, jnp.arange(n_dev, dtype=idx.dtype))
    w1p, w2p, w1tp = expanded_weights(w_first, w_second, n_dev, order)
    step = tok_rows // CHUNKS

    def rows(a, k):
        return a[k * step:(k + 1) * step]

    def forward(k):
        hidden = jnp.dot(rows(tokens, k), w1p, preferred_element_type=jnp.float32)
        hidden = hidden.astype(jnp.bfloat16)
        backed = jnp.dot(rows(cotangent, k), w2p, preferred_element_type=jnp.float32)
        return [hidden[:, m * part:(m + 1) * part] for m in range(n_dev)], backed

    def add(acc, val):
        return val if acc is None else acc + val

    pieces, backed = forward(0)
    moved = exchange(pieces, n_dev)
    gf_acc = gs_acc = None
    outs = []
    returned_prev = None
    for k in range(CHUNKS):
        masked = [
            jnp.where(moved[m] > 0, backed[:, m * part:(m + 1) * part], 0.0).astype(jnp.bfloat16)
            for m in range(n_dev)
        ]
        active = jnp.maximum(jnp.concatenate(moved, axis=1), jnp.zeros((), jnp.bfloat16))
        gs_k = lax.dot_general(
            active, rows(cotangent, k), (((0,), (0,)), ((), ())), preferred_element_type=jnp.float32
        )
        if k + 1 < CHUNKS:
            pieces, backed = forward(k + 1)
            tied = (masked, pieces, backed, gs_acc, gf_acc, outs)
            masked, pieces, backed, gs_acc, gf_acc, outs = lax.optimization_barrier(tied)
            moved = exchange(pieces, n_dev)
        gs_acc = add(gs_acc, gs_k)
        if returned_prev is not None:
            gt, gf = backward(returned_prev, tokens, k - 1, w1tp, step, n_dev, blk_local, sub)
            outs = outs + [gt]
            gf_acc = add(gf_acc, gf)
        returned_prev = jnp.concatenate(exchange(masked, n_dev), axis=1)
    gs6 = gs_acc.reshape(n_dev, blk_local, blk_local, sub, blk_local, bs)
    gsd = jnp.take(jnp.diagonal(gs6, axis1=1, axis2=4), order, axis=0)
    second_term = gsd.transpose(2, 0, 1, 4, 3).reshape(bs, blk_local, bs) * grad_scale
    grad_second = lax.psum_scatter(second_term, "dp", scatter_dimension=0, tiled=True)
    returned_prev, grad_second = lax.optimization_barrier((returned_prev, grad_second))
    gt, gf = backward(returned_prev, tokens, CHUNKS - 1, w1tp, step, n_dev, blk_local, sub)
    outs = outs + [gt]
    gf_acc = add(gf_acc, gf)

    grad_tokens = jnp.concatenate(outs, axis=0)
    first_term = jnp.take(gf_acc, order, axis=2).reshape(bs, blk_local, bs) * grad_scale
    grad_first = lax.psum_scatter(first_term, "dp", scatter_dimension=0, tiled=True)
    return (grad_tokens, grad_first.transpose(1, 0, 2), grad_second.transpose(1, 0, 2))


def backward(returned, tokens, k, w1tp, step, n_dev, blk_local, sub):
    x = tokens[k * step:(k + 1) * step]
    gt = jnp.dot(returned, w1tp, preferred_element_type=jnp.float32).astype(jnp.bfloat16)
    gf = jnp.einsum(
        "tmcbq,tbi->ibmcq",
        returned.reshape(step, n_dev, blk_local, blk_local, sub),
        x.reshape(step, blk_local, -1),
        preferred_element_type=jnp.float32,
    )
    return gt, gf


def solution(mesh):
    return jax.shard_map(
        shards,
        mesh=mesh,
        in_specs=(
            P(("groups", "dp"), "tensor"),
            P(("groups", "dp"), "tensor"),
            P("tensor", None, None),
            P("tensor", None, None),
        ),
        out_specs=(
            P(("groups", "dp"), "tensor"),
            P(("groups", "tensor"), "dp", None),
            P(("groups", "tensor"), "dp", None),
        ),
        check_vma=False,
    )
```

```python
import math

import jax
import jax.numpy as jnp
from jax import lax
from jax.sharding import PartitionSpec as P

NB = 16
CHUNKS = 4


def expanded_weights(w_first, w_second, n_dev, order):
    blk_local, bs, _ = w_first.shape
    sub = bs // NB
    feat = blk_local * bs
    eye = jnp.eye(blk_local, dtype=jnp.bool_)
    zero = jnp.zeros((), w_first.dtype)
    w1r = jnp.take(w_first.reshape(blk_local, bs, n_dev, blk_local, sub), order, axis=2)
    w1p = jnp.where(
        eye[:, None, None, None, :, None], w1r[:, :, :, :, None, :], zero
    ).reshape(feat, feat)
    w2r = jnp.take(w_second.reshape(blk_local, sub, n_dev, blk_local, bs), order, axis=2)
    w2r = w2r.transpose(0, 4, 2, 3, 1)
    w2p = jnp.where(
        eye[:, None, None, :, None, None], w2r[:, :, :, None, :, :], zero
    ).reshape(feat, feat)
    w1t = w1r.transpose(2, 3, 4, 0, 1)
    w1tp = jnp.where(
        eye[None, None, :, None, :, None], w1t[:, :, None, :, :, :], zero
    ).reshape(feat, feat)
    return w1p, w2p, w1tp


def exchange(pieces, n_dev):
    outs = [pieces[0]]
    for m in range(1, n_dev):
        outs.append(lax.ppermute(pieces[m], "tensor", [(i, i ^ m) for i in range(n_dev)]))
    return outs


def shards(tokens, cotangent, w_first, w_second):
    tok_rows = tokens.shape[0]
    blk_local, bs, _ = w_first.shape
    feat = blk_local * bs
    sub = bs // NB
    n_dev = lax.axis_size("tensor")
    part = feat // n_dev
    dp_count = lax.axis_size("dp")
    grad_scale = 1.0 / math.sqrt(tok_rows * dp_count)
    idx = lax.axis_index("tensor")
    order = jnp.bitwise_xor(idx, jnp.arange(n_dev, dtype=idx.dtype))
    w1p, w2p, w1tp = expanded_weights(w_first, w_second, n_dev, order)
    step = tok_rows // CHUNKS

    def rows(a, k):
        return a[k * step:(k + 1) * step]

    def forward(tok, cot, k):
        hidden = jnp.dot(rows(tok, k), w1p, preferred_element_type=jnp.float32)
        hidden = hidden.astype(jnp.bfloat16)
        backed = jnp.dot(rows(cot, k), w2p, preferred_element_type=jnp.float32)
        return [hidden[:, m * part:(m + 1) * part] for m in range(n_dev)], backed

    def add(acc, val):
        return val if acc is None else acc + val

    pieces, backed = forward(tokens, cotangent, 0)
    moved = exchange(pieces, n_dev)
    pieces_next, backed_next = forward(tokens, cotangent, 1)
    grad_tokens = jnp.zeros((tok_rows, feat), jnp.bfloat16)
    gf_acc = gs_acc = None
    returned = None
    grad_second = None
    for j in range(1, CHUNKS + 1):
        masked = [
            jnp.where(moved[m] > 0, backed[:, m * part:(m + 1) * part], 0.0).astype(jnp.bfloat16)
            for m in range(n_dev)
        ]
        tied = (masked, pieces_next, backed_next, moved, returned, tokens, cotangent,
                gs_acc, gf_acc, grad_tokens)
        (masked, pieces_next, backed_next, moved, returned, tokens, cotangent,
         gs_acc, gf_acc, grad_tokens) = lax.optimization_barrier(tied)
        moved_prev, returned_prev = moved, returned
        if j < CHUNKS:
            moved = exchange(pieces_next, n_dev)
            backed = backed_next
        returned = jnp.concatenate(exchange(masked, n_dev), axis=1)
        if j + 1 < CHUNKS:
            pieces_next, backed_next = forward(tokens, cotangent, j + 1)
        active = jnp.maximum(jnp.concatenate(moved_prev, axis=1), jnp.zeros((), jnp.bfloat16))
        gs_acc = add(gs_acc, lax.dot_general(
            active, rows(cotangent, j - 1), (((0,), (0,)), ((), ())),
            preferred_element_type=jnp.float32))
        if returned_prev is not None:
            gt, gf = backward(returned_prev, rows(tokens, j - 2), w1tp, n_dev, blk_local, sub)
            grad_tokens = lax.dynamic_update_slice(grad_tokens, gt, ((j - 2) * step, 0))
            gf_acc = add(gf_acc, gf)
        if j == CHUNKS:
            gs6 = gs_acc.reshape(n_dev, blk_local, blk_local, sub, blk_local, bs)
            gsd = jnp.take(jnp.diagonal(gs6, axis1=1, axis2=4), order, axis=0)
            second_term = gsd.transpose(4, 2, 0, 1, 3).reshape(blk_local, bs, bs) * grad_scale
            grad_second = lax.psum_scatter(second_term, "dp", scatter_dimension=1, tiled=True)
            returned, grad_second, tokens = lax.optimization_barrier((returned, grad_second, tokens))
    gt, gf = backward(returned, rows(tokens, CHUNKS - 1), w1tp, n_dev, blk_local, sub)
    grad_tokens = lax.dynamic_update_slice(grad_tokens, gt, ((CHUNKS - 1) * step, 0))
    gf_acc = add(gf_acc, gf)
    first_term = jnp.take(gf_acc, order, axis=2).reshape(blk_local, bs, bs) * grad_scale
    grad_first = lax.psum_scatter(first_term, "dp", scatter_dimension=1, tiled=True)
    return (grad_tokens, grad_first, grad_second)


def backward(returned, x, w1tp, n_dev, blk_local, sub):
    step = x.shape[0]
    gt = jnp.dot(returned, w1tp, preferred_element_type=jnp.float32).astype(jnp.bfloat16)
    gf = jnp.einsum(
        "tmcbq,tbi->bimcq",
        returned.reshape(step, n_dev, blk_local, blk_local, sub),
        x.reshape(step, blk_local, -1),
        preferred_element_type=jnp.float32,
    )
    return gt, gf


def solution(mesh):
    return jax.shard_map(
        shards,
        mesh=mesh,
        in_specs=(
            P(("groups", "dp"), "tensor"),
            P(("groups", "dp"), "tensor"),
            P("tensor", None, None),
            P("tensor", None, None),
        ),
        out_specs=(
            P(("groups", "dp"), "tensor"),
            P(("groups", "tensor"), "dp", None),
            P(("groups", "tensor"), "dp", None),
        ),
        check_vma=False,
    )
```

```python
import math

import jax
import jax.numpy as jnp
from jax import lax
from jax.sharding import PartitionSpec as P

NB = 16
CHUNKS = 4


def expanded_weights(w_first, w_second, n_dev, order):
    blk_local, bs, _ = w_first.shape
    sub = bs // NB
    feat = blk_local * bs
    eye = jnp.eye(blk_local, dtype=jnp.bool_)
    zero = jnp.zeros((), w_first.dtype)
    w1r = jnp.take(w_first.reshape(blk_local, bs, n_dev, blk_local, sub), order, axis=2)
    w1p = jnp.where(
        eye[:, None, None, None, :, None], w1r[:, :, :, :, None, :], zero
    ).reshape(feat, feat)
    w2r = jnp.take(w_second.reshape(blk_local, sub, n_dev, blk_local, bs), order, axis=2)
    w2r = w2r.transpose(0, 4, 2, 3, 1)
    w2p = jnp.where(
        eye[:, None, None, :, None, None], w2r[:, :, :, None, :, :], zero
    ).reshape(feat, feat)
    w1t = w1r.transpose(2, 3, 4, 0, 1)
    w1tp = jnp.where(
        eye[None, None, :, None, :, None], w1t[:, :, None, :, :, :], zero
    ).reshape(feat, feat)
    return w1p, w2p, w1tp


def exchange(pieces, n_dev):
    outs = [pieces[0]]
    for m in range(1, n_dev):
        outs.append(lax.ppermute(pieces[m], "tensor", [(i, i ^ m) for i in range(n_dev)]))
    return outs


def shards(tokens, cotangent, w_first, w_second):
    tok_rows = tokens.shape[0]
    blk_local, bs, _ = w_first.shape
    feat = blk_local * bs
    sub = bs // NB
    part = feat // lax.axis_size("tensor")
    n_dev = lax.axis_size("tensor")
    dp_count = lax.axis_size("dp")
    grad_scale = 1.0 / math.sqrt(tok_rows * dp_count)
    idx = lax.axis_index("tensor")
    order = jnp.bitwise_xor(idx, jnp.arange(n_dev, dtype=idx.dtype))
    w1p, w2p, w1tp = expanded_weights(w_first, w_second, n_dev, order)
    step = tok_rows // CHUNKS

    eye = jnp.eye(blk_local, dtype=jnp.bool_)
    gf_acc = None
    gs_acc = None
    outs = []
    pending = []
    for k in range(CHUNKS):
        x = tokens[k * step:(k + 1) * step]
        cot = cotangent[k * step:(k + 1) * step]
        hidden = jnp.dot(x, w1p, preferred_element_type=jnp.float32).astype(jnp.bfloat16)
        backed = jnp.dot(cot, w2p, preferred_element_type=jnp.float32)
        moved = exchange([hidden[:, m * part:(m + 1) * part] for m in range(n_dev)], n_dev)
        masked = [
            jnp.where(moved[m] > 0, backed[:, m * part:(m + 1) * part], 0.0).astype(jnp.bfloat16)
            for m in range(n_dev)
        ]
        active = jnp.maximum(jnp.concatenate(moved, axis=1), jnp.zeros((), jnp.bfloat16))
        gs = lax.dot_general(
            active, cot, (((0,), (0,)), ((), ())), preferred_element_type=jnp.float32
        )
        gs_acc = gs if gs_acc is None else gs_acc + gs
        if len(pending) == 2:
            masked, done = lax.optimization_barrier((masked, pending.pop(0)))
            outs.append(done[0])
            gf_acc = done[1] if gf_acc is None else gf_acc + done[1]
        returned = jnp.concatenate(exchange(masked, n_dev), axis=1)
        gt = jnp.dot(returned, w1tp, preferred_element_type=jnp.float32).astype(jnp.bfloat16)
        gf = lax.dot_general(
            x, returned, (((0,), (0,)), ((), ())), preferred_element_type=jnp.float32
        )
        pending.append((gt, gf))
    for gt, gf in pending:
        outs.append(gt)
        gf_acc = gf if gf_acc is None else gf_acc + gf

    grad_tokens = jnp.concatenate(outs, axis=0)
    gs6 = gs_acc.reshape(n_dev, blk_local, blk_local, sub, blk_local, bs)
    gsd = jnp.sum(jnp.where(eye[None, :, None, None, :, None], gs6, 0.0), axis=4)
    gsd = jnp.take(gsd, order, axis=0)
    second_term = gsd.transpose(3, 0, 2, 1, 4).reshape(bs, blk_local, bs) * grad_scale
    grad_second = lax.psum_scatter(second_term, "dp", scatter_dimension=0, tiled=True)
    gf_acc, grad_second = lax.optimization_barrier((gf_acc, grad_second))
    gf6 = gf_acc.reshape(blk_local, bs, n_dev, blk_local, blk_local, sub)
    gfd = jnp.sum(jnp.where(eye[:, None, None, None, :, None], gf6, 0.0), axis=4)
    gfd = jnp.take(gfd, order, axis=2)
    first_term = gfd.transpose(1, 0, 2, 3, 4).reshape(bs, blk_local, bs) * grad_scale
    grad_first = lax.psum_scatter(first_term, "dp", scatter_dimension=0, tiled=True)
    return (grad_tokens, grad_first.transpose(1, 0, 2), grad_second.transpose(1, 0, 2))


def solution(mesh):
    return jax.shard_map(
        shards,
        mesh=mesh,
        in_specs=(
            P(("groups", "dp"), "tensor"),
            P(("groups", "dp"), "tensor"),
            P("tensor", None, None),
            P("tensor", None, None),
        ),
        out_specs=(
            P(("groups", "dp"), "tensor"),
            P(("groups", "tensor"), "dp", None),
            P(("groups", "tensor"), "dp", None),
        ),
        check_vma=False,
    )
```

```python
import math

import jax
import jax.numpy as jnp
from jax import lax
from jax.sharding import PartitionSpec as P

NB = 16
CHUNKS = 4


def expanded_weights(w_first, w_second, n_dev, order):
    blk_local, bs, _ = w_first.shape
    sub = bs // NB
    feat = blk_local * bs
    eye = jnp.eye(blk_local, dtype=jnp.bool_)
    zero = jnp.zeros((), w_first.dtype)
    w1r = jnp.take(w_first.reshape(blk_local, bs, n_dev, blk_local, sub), order, axis=2)
    w1p = jnp.where(
        eye[:, None, None, None, :, None], w1r[:, :, :, :, None, :], zero
    ).reshape(feat, feat)
    w2r = jnp.take(w_second.reshape(blk_local, sub, n_dev, blk_local, bs), order, axis=2)
    w2r = w2r.transpose(0, 4, 2, 3, 1)
    w2p = jnp.where(
        eye[:, None, None, :, None, None], w2r[:, :, :, None, :, :], zero
    ).reshape(feat, feat)
    w1t = w1r.transpose(2, 3, 4, 0, 1)
    w1tp = jnp.where(
        eye[None, None, :, None, :, None], w1t[:, :, None, :, :, :], zero
    ).reshape(feat, feat)
    return w1p, w2p, w1tp


def exchange(pieces, n_dev):
    outs = [pieces[0]]
    for m in range(1, n_dev):
        outs.append(lax.ppermute(pieces[m], "tensor", [(i, i ^ m) for i in range(n_dev)]))
    return outs


def shards(tokens, cotangent, w_first, w_second):
    tok_rows = tokens.shape[0]
    blk_local, bs, _ = w_first.shape
    feat = blk_local * bs
    sub = bs // NB
    part = feat // lax.axis_size("tensor")
    n_dev = lax.axis_size("tensor")
    dp_count = lax.axis_size("dp")
    grad_scale = 1.0 / math.sqrt(tok_rows * dp_count)
    idx = lax.axis_index("tensor")
    order = jnp.bitwise_xor(idx, jnp.arange(n_dev, dtype=idx.dtype))
    w1p, w2p, w1tp = expanded_weights(w_first, w_second, n_dev, order)
    step = tok_rows // CHUNKS

    eye = jnp.eye(blk_local, dtype=jnp.bool_)
    gf_acc = None
    gs_acc = None
    grad_tokens = jnp.zeros((tok_rows, feat), jnp.bfloat16)
    pending = []
    for k in range(CHUNKS):
        x = tokens[k * step:(k + 1) * step]
        cot = cotangent[k * step:(k + 1) * step]
        hidden = jnp.dot(x, w1p, preferred_element_type=jnp.float32).astype(jnp.bfloat16)
        backed = jnp.dot(cot, w2p, preferred_element_type=jnp.float32)
        moved = exchange([hidden[:, m * part:(m + 1) * part] for m in range(n_dev)], n_dev)
        masked = [
            jnp.where(moved[m] > 0, backed[:, m * part:(m + 1) * part], 0.0).astype(jnp.bfloat16)
            for m in range(n_dev)
        ]
        active = jnp.maximum(jnp.concatenate(moved, axis=1), jnp.zeros((), jnp.bfloat16))
        gs = lax.dot_general(
            active, cot, (((0,), (0,)), ((), ())), preferred_element_type=jnp.float32
        )
        gs_acc = gs if gs_acc is None else gs_acc + gs
        if len(pending) == 2:
            masked, done = lax.optimization_barrier((masked, pending.pop(0)))
            grad_tokens = lax.dynamic_update_slice(grad_tokens, done[0], (done[2], 0))
            gf_acc = done[1] if gf_acc is None else gf_acc + done[1]
        returned = jnp.concatenate(exchange(masked, n_dev), axis=1)
        gt = jnp.dot(returned, w1tp, preferred_element_type=jnp.float32).astype(jnp.bfloat16)
        gf = lax.dot_general(
            x, returned, (((0,), (0,)), ((), ())), preferred_element_type=jnp.float32
        )
        pending.append((gt, gf, k * step))
    for gt, gf, at in pending:
        grad_tokens = lax.dynamic_update_slice(grad_tokens, gt, (at, 0))
        gf_acc = gf if gf_acc is None else gf_acc + gf

    gs6 = gs_acc.reshape(n_dev, blk_local, blk_local, sub, blk_local, bs)
    gsd = jnp.sum(jnp.where(eye[None, :, None, None, :, None], gs6, 0.0), axis=4)
    gsd = jnp.take(gsd, order, axis=0)
    second_term = gsd.transpose(3, 0, 2, 1, 4).reshape(bs, blk_local, bs) * grad_scale
    grad_second = lax.psum_scatter(second_term, "dp", scatter_dimension=0, tiled=True)
    gf_acc, grad_second = lax.optimization_barrier((gf_acc, grad_second))
    gf6 = gf_acc.reshape(blk_local, bs, n_dev, blk_local, blk_local, sub)
    gfd = jnp.sum(jnp.where(eye[:, None, None, None, :, None], gf6, 0.0), axis=4)
    gfd = jnp.take(gfd, order, axis=2)
    first_term = gfd.transpose(1, 0, 2, 3, 4).reshape(bs, blk_local, bs) * grad_scale
    grad_first = lax.psum_scatter(first_term, "dp", scatter_dimension=0, tiled=True)
    return (grad_tokens, grad_first.transpose(1, 0, 2), grad_second.transpose(1, 0, 2))


def solution(mesh):
    return jax.shard_map(
        shards,
        mesh=mesh,
        in_specs=(
            P(("groups", "dp"), "tensor"),
            P(("groups", "dp"), "tensor"),
            P("tensor", None, None),
            P("tensor", None, None),
        ),
        out_specs=(
            P(("groups", "dp"), "tensor"),
            P(("groups", "tensor"), "dp", None),
            P(("groups", "tensor"), "dp", None),
        ),
        check_vma=False,
    )
```

```python
import math

import jax
import jax.numpy as jnp
from jax import lax
from jax.sharding import PartitionSpec as P

NB = 16
CHUNKS = 4


def expanded_weights(w_first, w_second, n_dev, order):
    blk_local, bs, _ = w_first.shape
    sub = bs // NB
    feat = blk_local * bs
    eye = jnp.eye(blk_local, dtype=jnp.bool_)
    zero = jnp.zeros((), w_first.dtype)
    w1r = jnp.take(w_first.reshape(blk_local, bs, n_dev, blk_local, sub), order, axis=2)
    w1p = jnp.where(
        eye[:, None, None, None, :, None], w1r[:, :, :, :, None, :], zero
    ).reshape(feat, feat)
    w2r = jnp.take(w_second.reshape(blk_local, sub, n_dev, blk_local, bs), order, axis=2)
    w2r = w2r.transpose(0, 4, 2, 3, 1)
    w2p = jnp.where(
        eye[:, None, None, :, None, None], w2r[:, :, :, None, :, :], zero
    ).reshape(feat, feat)
    w1t = w1r.transpose(2, 3, 4, 0, 1)
    w1tp = jnp.where(
        eye[None, None, :, None, :, None], w1t[:, :, None, :, :, :], zero
    ).reshape(feat, feat)
    return w1p, w2p, w1tp


def exchange(pieces, n_dev):
    outs = [pieces[0]]
    for m in range(1, n_dev):
        outs.append(lax.ppermute(pieces[m], "tensor", [(i, i ^ m) for i in range(n_dev)]))
    return outs


def dp_reduce_scatter(x):
    n = lax.axis_size("dp")
    didx = lax.axis_index("dp")
    blocks = x.reshape((n, x.shape[0] // n) + x.shape[1:])
    acc = lax.dynamic_index_in_dim(blocks, didx, axis=0, keepdims=False)
    for m in range(1, n):
        send = lax.dynamic_index_in_dim(blocks, jnp.bitwise_xor(didx, m), axis=0, keepdims=False)
        acc = acc + lax.ppermute(send, "dp", [(i, i ^ m) for i in range(n)])
    return acc


def shards(tokens, cotangent, w_first, w_second):
    tok_rows = tokens.shape[0]
    blk_local, bs, _ = w_first.shape
    feat = blk_local * bs
    sub = bs // NB
    part = feat // lax.axis_size("tensor")
    n_dev = lax.axis_size("tensor")
    dp_count = lax.axis_size("dp")
    grad_scale = 1.0 / math.sqrt(tok_rows * dp_count)
    idx = lax.axis_index("tensor")
    order = jnp.bitwise_xor(idx, jnp.arange(n_dev, dtype=idx.dtype))
    w1p, w2p, w1tp = expanded_weights(w_first, w_second, n_dev, order)
    step = tok_rows // CHUNKS

    eye = jnp.eye(blk_local, dtype=jnp.bool_)
    gf_acc = None
    gs_acc = None
    grad_tokens = jnp.zeros((tok_rows, feat), jnp.bfloat16)
    pending = []
    for k in range(CHUNKS):
        x = tokens[k * step:(k + 1) * step]
        cot = cotangent[k * step:(k + 1) * step]
        hidden = jnp.dot(x, w1p, preferred_element_type=jnp.float32).astype(jnp.bfloat16)
        backed = jnp.dot(cot, w2p, preferred_element_type=jnp.float32)
        moved = exchange([hidden[:, m * part:(m + 1) * part] for m in range(n_dev)], n_dev)
        masked = [
            jnp.where(moved[m] > 0, backed[:, m * part:(m + 1) * part], 0.0).astype(jnp.bfloat16)
            for m in range(n_dev)
        ]
        active = jnp.maximum(jnp.concatenate(moved, axis=1), jnp.zeros((), jnp.bfloat16))
        gs = lax.dot_general(
            active, cot, (((0,), (0,)), ((), ())), preferred_element_type=jnp.float32
        )
        gs_acc = gs if gs_acc is None else gs_acc + gs
        if len(pending) == 2:
            masked, done = lax.optimization_barrier((masked, pending.pop(0)))
            grad_tokens = lax.dynamic_update_slice(grad_tokens, done[0], (done[2], 0))
            gf_acc = done[1] if gf_acc is None else gf_acc + done[1]
        returned = jnp.concatenate(exchange(masked, n_dev), axis=1)
        gt = jnp.dot(returned, w1tp, preferred_element_type=jnp.float32).astype(jnp.bfloat16)
        gf = lax.dot_general(
            x, returned, (((0,), (0,)), ((), ())), preferred_element_type=jnp.float32
        )
        pending.append((gt, gf, k * step))
    for gt, gf, at in pending:
        grad_tokens = lax.dynamic_update_slice(grad_tokens, gt, (at, 0))
        gf_acc = gf if gf_acc is None else gf_acc + gf

    gs6 = gs_acc.reshape(n_dev, blk_local, blk_local, sub, blk_local, bs)
    gsd = jnp.sum(jnp.where(eye[None, :, None, None, :, None], gs6, 0.0), axis=4)
    gsd = jnp.take(gsd, order, axis=0)
    second_term = gsd.transpose(3, 0, 2, 1, 4).reshape(bs, blk_local, bs) * grad_scale
    grad_second = lax.psum_scatter(second_term, "dp", scatter_dimension=0, tiled=True)
    gf_acc, grad_second = lax.optimization_barrier((gf_acc, grad_second))
    gf6 = gf_acc.reshape(blk_local, bs, n_dev, blk_local, blk_local, sub)
    gfd = jnp.sum(jnp.where(eye[:, None, None, None, :, None], gf6, 0.0), axis=4)
    gfd = jnp.take(gfd, order, axis=2)
    first_term = gfd.transpose(1, 0, 2, 3, 4).reshape(bs, blk_local, bs) * grad_scale
    grad_first = dp_reduce_scatter(first_term)
    return (grad_tokens, grad_first.transpose(1, 0, 2), grad_second.transpose(1, 0, 2))


def solution(mesh):
    return jax.shard_map(
        shards,
        mesh=mesh,
        in_specs=(
            P(("groups", "dp"), "tensor"),
            P(("groups", "dp"), "tensor"),
            P("tensor", None, None),
            P("tensor", None, None),
        ),
        out_specs=(
            P(("groups", "dp"), "tensor"),
            P(("groups", "tensor"), "dp", None),
            P(("groups", "tensor"), "dp", None),
        ),
        check_vma=False,
    )
```

```python
import math

import jax
import jax.numpy as jnp
from jax import lax
from jax.sharding import PartitionSpec as P

NB = 16
SIZES = (2, 2, 2, 1, 1)


def expanded_weights(w_first, w_second, n_dev, order):
    blk_local, bs, _ = w_first.shape
    sub = bs // NB
    feat = blk_local * bs
    eye = jnp.eye(blk_local, dtype=jnp.bool_)
    zero = jnp.zeros((), w_first.dtype)
    w1r = jnp.take(w_first.reshape(blk_local, bs, n_dev, blk_local, sub), order, axis=2)
    w1p = jnp.where(
        eye[:, None, None, None, :, None], w1r[:, :, :, :, None, :], zero
    ).reshape(feat, feat)
    w2r = jnp.take(w_second.reshape(blk_local, sub, n_dev, blk_local, bs), order, axis=2)
    w2r = w2r.transpose(0, 4, 2, 3, 1)
    w2p = jnp.where(
        eye[:, None, None, :, None, None], w2r[:, :, :, None, :, :], zero
    ).reshape(feat, feat)
    w1t = w1r.transpose(2, 3, 4, 0, 1)
    w1tp = jnp.where(
        eye[None, None, :, None, :, None], w1t[:, :, None, :, :, :], zero
    ).reshape(feat, feat)
    return w1p, w2p, w1tp


def exchange(pieces, n_dev):
    outs = [pieces[0]]
    for m in range(1, n_dev):
        outs.append(lax.ppermute(pieces[m], "tensor", [(i, i ^ m) for i in range(n_dev)]))
    return outs


def dp_reduce_scatter(x):
    n = lax.axis_size("dp")
    didx = lax.axis_index("dp")
    blocks = x.reshape((n, x.shape[0] // n) + x.shape[1:])
    acc = lax.dynamic_index_in_dim(blocks, didx, axis=0, keepdims=False)
    for m in range(1, n):
        send = lax.dynamic_index_in_dim(blocks, jnp.bitwise_xor(didx, m), axis=0, keepdims=False)
        acc = acc + lax.ppermute(send, "dp", [(i, i ^ m) for i in range(n)])
    return acc


def shards(tokens, cotangent, w_first, w_second):
    tok_rows = tokens.shape[0]
    blk_local, bs, _ = w_first.shape
    feat = blk_local * bs
    sub = bs // NB
    part = feat // lax.axis_size("tensor")
    n_dev = lax.axis_size("tensor")
    dp_count = lax.axis_size("dp")
    grad_scale = 1.0 / math.sqrt(tok_rows * dp_count)
    idx = lax.axis_index("tensor")
    order = jnp.bitwise_xor(idx, jnp.arange(n_dev, dtype=idx.dtype))
    w1p, w2p, w1tp = expanded_weights(w_first, w_second, n_dev, order)
    unit = tok_rows // sum(SIZES)
    offsets = [unit * sum(SIZES[:k]) for k in range(len(SIZES) + 1)]

    eye = jnp.eye(blk_local, dtype=jnp.bool_)
    gf_acc = None
    gs_acc = None
    grad_tokens = jnp.zeros((tok_rows, feat), jnp.bfloat16)
    pending = []
    last = len(SIZES) - 1
    for k in range(len(SIZES)):
        x = tokens[offsets[k]:offsets[k + 1]]
        cot = cotangent[offsets[k]:offsets[k + 1]]
        hidden = jnp.dot(x, w1p, preferred_element_type=jnp.float32).astype(jnp.bfloat16)
        backed = jnp.dot(cot, w2p, preferred_element_type=jnp.float32)
        moved = exchange([hidden[:, m * part:(m + 1) * part] for m in range(n_dev)], n_dev)
        masked = [
            jnp.where(moved[m] > 0, backed[:, m * part:(m + 1) * part], 0.0).astype(jnp.bfloat16)
            for m in range(n_dev)
        ]
        active = jnp.maximum(jnp.concatenate(moved, axis=1), jnp.zeros((), jnp.bfloat16))
        gs = lax.dot_general(
            active, cot, (((0,), (0,)), ((), ())), preferred_element_type=jnp.float32
        )
        gs_acc = gs if gs_acc is None else gs_acc + gs
        if len(pending) == 2:
            masked, done = lax.optimization_barrier((masked, pending.pop(0)))
            grad_tokens = lax.dynamic_update_slice(grad_tokens, done[0], (done[2], 0))
            gf_acc = done[1] if gf_acc is None else gf_acc + done[1]
        returned = jnp.concatenate(exchange(masked, n_dev), axis=1)
        gt = jnp.dot(returned, w1tp, preferred_element_type=jnp.float32).astype(jnp.bfloat16)
        if k < last:
            gf = lax.dot_general(
                x, returned, (((0,), (0,)), ((), ())), preferred_element_type=jnp.float32
            )
        else:
            gf = jnp.einsum(
                "tmcbq,tbi->bimcq",
                returned.reshape(-1, n_dev, blk_local, blk_local, sub),
                x.reshape(-1, blk_local, bs),
                preferred_element_type=jnp.float32,
            )
        pending.append((gt, gf, offsets[k]))
    gf_last = None
    for gt, gf, at in pending:
        grad_tokens = lax.dynamic_update_slice(grad_tokens, gt, (at, 0))
        if at == offsets[last]:
            gf_last = gf
        else:
            gf_acc = gf if gf_acc is None else gf_acc + gf

    gs6 = gs_acc.reshape(n_dev, blk_local, blk_local, sub, blk_local, bs)
    gsd = jnp.sum(jnp.where(eye[None, :, None, None, :, None], gs6, 0.0), axis=4)
    gsd = jnp.take(gsd, order, axis=0)
    second_term = gsd.transpose(3, 0, 2, 1, 4).reshape(bs, blk_local, bs) * grad_scale
    grad_second = lax.psum_scatter(second_term, "dp", scatter_dimension=0, tiled=True)
    gf_acc, grad_second = lax.optimization_barrier((gf_acc, grad_second))
    gf6 = gf_acc.reshape(blk_local, bs, n_dev, blk_local, blk_local, sub)
    gfd = jnp.sum(jnp.where(eye[:, None, None, None, :, None], gf6, 0.0), axis=4)
    gfd = jnp.take(gfd + gf_last, order, axis=2)
    first_term = gfd.transpose(1, 0, 2, 3, 4).reshape(bs, blk_local, bs) * grad_scale
    grad_first = dp_reduce_scatter(first_term)
    return (grad_tokens, grad_first.transpose(1, 0, 2), grad_second.transpose(1, 0, 2))


def solution(mesh):
    return jax.shard_map(
        shards,
        mesh=mesh,
        in_specs=(
            P(("groups", "dp"), "tensor"),
            P(("groups", "dp"), "tensor"),
            P("tensor", None, None),
            P("tensor", None, None),
        ),
        out_specs=(
            P(("groups", "dp"), "tensor"),
            P(("groups", "tensor"), "dp", None),
            P(("groups", "tensor"), "dp", None),
        ),
        check_vma=False,
    )
```

```python
import math

import jax
import jax.numpy as jnp
from jax import lax
from jax.sharding import PartitionSpec as P

NB = 16
CHUNKS = 4


def expanded_weights(w_first, w_second, n_dev, order):
    blk_local, bs, _ = w_first.shape
    sub = bs // NB
    feat = blk_local * bs
    eye = jnp.eye(blk_local, dtype=jnp.bool_)
    zero = jnp.zeros((), w_first.dtype)
    w1r = jnp.take(w_first.reshape(blk_local, bs, n_dev, blk_local, sub), order, axis=2)
    w1p = jnp.where(
        eye[:, None, None, None, :, None], w1r[:, :, :, :, None, :], zero
    ).reshape(feat, feat)
    w2r = jnp.take(w_second.reshape(blk_local, sub, n_dev, blk_local, bs), order, axis=2)
    w2r = w2r.transpose(0, 4, 2, 3, 1)
    w2p = jnp.where(
        eye[:, None, None, :, None, None], w2r[:, :, :, None, :, :], zero
    ).reshape(feat, feat)
    w1t = w1r.transpose(2, 3, 4, 0, 1)
    w1tp = jnp.where(
        eye[None, None, :, None, :, None], w1t[:, :, None, :, :, :], zero
    ).reshape(feat, feat)
    return w1p, w2p, w1tp


def exchange(pieces, n_dev):
    outs = [pieces[0]]
    for m in range(1, n_dev):
        outs.append(lax.ppermute(pieces[m], "tensor", [(i, i ^ m) for i in range(n_dev)]))
    return outs


def dp_reduce_scatter(x):
    n = lax.axis_size("dp")
    didx = lax.axis_index("dp")
    blocks = x.reshape((n, x.shape[0] // n) + x.shape[1:])
    acc = lax.dynamic_index_in_dim(blocks, didx, axis=0, keepdims=False)
    for m in range(1, n):
        send = lax.dynamic_index_in_dim(blocks, jnp.bitwise_xor(didx, m), axis=0, keepdims=False)
        acc = acc + lax.ppermute(send, "dp", [(i, i ^ m) for i in range(n)])
    return acc


def shards(tokens, cotangent, w_first, w_second):
    tok_rows = tokens.shape[0]
    blk_local, bs, _ = w_first.shape
    feat = blk_local * bs
    sub = bs // NB
    part = feat // lax.axis_size("tensor")
    n_dev = lax.axis_size("tensor")
    dp_count = lax.axis_size("dp")
    grad_scale = 1.0 / math.sqrt(tok_rows * dp_count)
    idx = lax.axis_index("tensor")
    order = jnp.bitwise_xor(idx, jnp.arange(n_dev, dtype=idx.dtype))
    w1p, w2p, w1tp = expanded_weights(w_first, w_second, n_dev, order)
    step = tok_rows // CHUNKS

    eye = jnp.eye(blk_local, dtype=jnp.bool_)
    gf_acc = None
    gs_acc = None
    grad_tokens = jnp.zeros((tok_rows, feat), jnp.bfloat16)
    pending = []
    for k in range(CHUNKS):
        x = tokens[k * step:(k + 1) * step]
        cot = cotangent[k * step:(k + 1) * step]
        hidden = jnp.dot(x, w1p, preferred_element_type=jnp.float32).astype(jnp.bfloat16)
        backed = jnp.dot(cot, w2p, preferred_element_type=jnp.float32)
        moved = exchange([hidden[:, m * part:(m + 1) * part] for m in range(n_dev)], n_dev)
        masked = [
            jnp.where(moved[m] > 0, backed[:, m * part:(m + 1) * part], 0.0).astype(jnp.bfloat16)
            for m in range(n_dev)
        ]
        active = jnp.maximum(jnp.concatenate(moved, axis=1), jnp.zeros((), jnp.bfloat16))
        gs = lax.dot_general(
            active, cot, (((0,), (0,)), ((), ())), preferred_element_type=jnp.float32
        )
        gs_acc = gs if gs_acc is None else gs_acc + gs
        if len(pending) == 2:
            masked, done = lax.optimization_barrier((masked, pending.pop(0)))
            grad_tokens = lax.dynamic_update_slice(grad_tokens, done[0], (done[2], 0))
            gf_acc = done[1] if gf_acc is None else gf_acc + done[1]
        if k + 1 < CHUNKS:
            returned = jnp.concatenate(exchange(masked, n_dev), axis=1)
            gt = jnp.dot(returned, w1tp, preferred_element_type=jnp.float32).astype(jnp.bfloat16)
            gf = lax.dot_general(
                x, returned, (((0,), (0,)), ((), ())), preferred_element_type=jnp.float32
            )
        else:
            gt = None
            gf = []
            for m, piece in enumerate(exchange(masked, n_dev)):
                term = jnp.dot(piece, w1tp[m * part:(m + 1) * part],
                               preferred_element_type=jnp.float32)
                gt = term if gt is None else gt + term
                g = lax.dot_general(
                    x, piece, (((0,), (0,)), ((), ())), preferred_element_type=jnp.float32
                ).reshape(blk_local, bs, blk_local, blk_local, sub)
                gf.append(jnp.sum(jnp.where(eye[:, None, None, :, None], g, 0.0), axis=3))
            gt = gt.astype(jnp.bfloat16)
            gf = jnp.stack(gf, axis=2)
        pending.append((gt, gf, k * step))
    gf_last = None
    for gt, gf, at in pending:
        grad_tokens = lax.dynamic_update_slice(grad_tokens, gt, (at, 0))
        if at == (CHUNKS - 1) * step:
            gf_last = gf
        else:
            gf_acc = gf if gf_acc is None else gf_acc + gf

    gs6 = gs_acc.reshape(n_dev, blk_local, blk_local, sub, blk_local, bs)
    gsd = jnp.sum(jnp.where(eye[None, :, None, None, :, None], gs6, 0.0), axis=4)
    gsd = jnp.take(gsd, order, axis=0)
    second_term = gsd.transpose(3, 0, 2, 1, 4).reshape(bs, blk_local, bs) * grad_scale
    grad_second = lax.psum_scatter(second_term, "dp", scatter_dimension=0, tiled=True)
    gf_acc, grad_second = lax.optimization_barrier((gf_acc, grad_second))
    gf6 = gf_acc.reshape(blk_local, bs, n_dev, blk_local, blk_local, sub)
    gfd = jnp.sum(jnp.where(eye[:, None, None, None, :, None], gf6, 0.0), axis=4)
    gfd = jnp.take(gfd + gf_last, order, axis=2)
    first_term = gfd.transpose(1, 0, 2, 3, 4).reshape(bs, blk_local, bs) * grad_scale
    grad_first = dp_reduce_scatter(first_term)
    return (grad_tokens, grad_first.transpose(1, 0, 2), grad_second.transpose(1, 0, 2))


def solution(mesh):
    return jax.shard_map(
        shards,
        mesh=mesh,
        in_specs=(
            P(("groups", "dp"), "tensor"),
            P(("groups", "dp"), "tensor"),
            P("tensor", None, None),
            P("tensor", None, None),
        ),
        out_specs=(
            P(("groups", "dp"), "tensor"),
            P(("groups", "tensor"), "dp", None),
            P(("groups", "tensor"), "dp", None),
        ),
        check_vma=False,
    )
```

```python
import math

import jax
import jax.numpy as jnp
from jax import lax
from jax.sharding import PartitionSpec as P

NB = 16
CHUNKS = 4


def expanded_weights(w_first, w_second, n_dev, order):
    blk_local, bs, _ = w_first.shape
    sub = bs // NB
    feat = blk_local * bs
    eye = jnp.eye(blk_local, dtype=jnp.bool_)
    zero = jnp.zeros((), w_first.dtype)
    w1r = jnp.take(w_first.reshape(blk_local, bs, n_dev, blk_local, sub), order, axis=2)
    w1p = jnp.where(
        eye[:, None, None, None, :, None], w1r[:, :, :, :, None, :], zero
    ).reshape(feat, feat)
    w2r = jnp.take(w_second.reshape(blk_local, sub, n_dev, blk_local, bs), order, axis=2)
    w2r = w2r.transpose(0, 4, 2, 3, 1)
    w2p = jnp.where(
        eye[:, None, None, :, None, None], w2r[:, :, :, None, :, :], zero
    ).reshape(feat, feat)
    w1t = w1r.transpose(2, 3, 4, 0, 1)
    w1tp = jnp.where(
        eye[None, None, :, None, :, None], w1t[:, :, None, :, :, :], zero
    ).reshape(feat, feat)
    return w1p, w2p, w1tp


def exchange(pieces, n_dev):
    outs = [pieces[0]]
    for m in range(1, n_dev):
        outs.append(lax.ppermute(pieces[m], "tensor", [(i, i ^ m) for i in range(n_dev)]))
    return outs


def dp_reduce_scatter(x):
    n = lax.axis_size("dp")
    didx = lax.axis_index("dp")
    blocks = x.reshape((n, x.shape[0] // n) + x.shape[1:])
    acc = lax.dynamic_index_in_dim(blocks, didx, axis=0, keepdims=False)
    for m in range(1, n):
        send = lax.dynamic_index_in_dim(blocks, jnp.bitwise_xor(didx, m), axis=0, keepdims=False)
        acc = acc + lax.ppermute(send, "dp", [(i, i ^ m) for i in range(n)])
    return acc


def shards(tokens, cotangent, w_first, w_second):
    tok_rows = tokens.shape[0]
    blk_local, bs, _ = w_first.shape
    feat = blk_local * bs
    sub = bs // NB
    part = feat // lax.axis_size("tensor")
    n_dev = lax.axis_size("tensor")
    dp_count = lax.axis_size("dp")
    grad_scale = 1.0 / math.sqrt(tok_rows * dp_count)
    idx = lax.axis_index("tensor")
    order = jnp.bitwise_xor(idx, jnp.arange(n_dev, dtype=idx.dtype))
    w1p, w2p, w1tp = expanded_weights(w_first, w_second, n_dev, order)
    step = tok_rows // CHUNKS

    eye = jnp.eye(blk_local, dtype=jnp.bool_)
    gf_acc = None
    gs_acc = None
    grad_tokens = jnp.zeros((tok_rows, feat), jnp.bfloat16)
    pending = []
    for k in range(CHUNKS):
        x = tokens[k * step:(k + 1) * step]
        cot = cotangent[k * step:(k + 1) * step]
        hidden = jnp.dot(x, w1p, preferred_element_type=jnp.float32).astype(jnp.bfloat16)
        backed = jnp.dot(cot, w2p, preferred_element_type=jnp.float32)
        moved = exchange([hidden[:, m * part:(m + 1) * part] for m in range(n_dev)], n_dev)
        masked = [
            jnp.where(moved[m] > 0, backed[:, m * part:(m + 1) * part], 0.0).astype(jnp.bfloat16)
            for m in range(n_dev)
        ]
        active = jnp.maximum(jnp.concatenate(moved, axis=1), jnp.zeros((), jnp.bfloat16))
        gs = lax.dot_general(
            active, cot, (((0,), (0,)), ((), ())), preferred_element_type=jnp.float32
        )
        gs_acc = gs if gs_acc is None else gs_acc + gs
        if len(pending) == 2:
            masked, done = lax.optimization_barrier((masked, pending.pop(0)))
            grad_tokens = lax.dynamic_update_slice(grad_tokens, done[0], (done[2], 0))
            gf_acc = done[1] if gf_acc is None else gf_acc + done[1]
        returned = jnp.concatenate(exchange(masked, n_dev), axis=1)
        gt = jnp.dot(returned, w1tp, preferred_element_type=jnp.float32).astype(jnp.bfloat16)
        gf = lax.dot_general(
            x, returned, (((0,), (0,)), ((), ())), preferred_element_type=jnp.float32
        )
        pending.append((gt, gf, k * step))
    for gt, gf, at in pending:
        grad_tokens = lax.dynamic_update_slice(grad_tokens, gt, (at, 0))
        gf_acc = gf if gf_acc is None else gf_acc + gf

    gs6 = gs_acc.reshape(n_dev, blk_local, blk_local, sub, blk_local, bs)
    gsd = jnp.sum(jnp.where(eye[None, :, None, None, :, None], gs6, 0.0), axis=4)
    gsd = jnp.take(gsd, order, axis=0)
    second_term = gsd.transpose(3, 0, 2, 1, 4).reshape(bs, blk_local, bs) * grad_scale
    grad_second = dp_reduce_scatter(second_term)
    gf_acc, grad_second = lax.optimization_barrier((gf_acc, grad_second))
    gf6 = gf_acc.reshape(blk_local, bs, n_dev, blk_local, blk_local, sub)
    gfd = jnp.sum(jnp.where(eye[:, None, None, None, :, None], gf6, 0.0), axis=4)
    gfd = jnp.take(gfd, order, axis=2)
    first_term = gfd.transpose(1, 0, 2, 3, 4).reshape(bs, blk_local, bs) * grad_scale
    grad_first = dp_reduce_scatter(first_term)
    return (grad_tokens, grad_first.transpose(1, 0, 2), grad_second.transpose(1, 0, 2))


def solution(mesh):
    return jax.shard_map(
        shards,
        mesh=mesh,
        in_specs=(
            P(("groups", "dp"), "tensor"),
            P(("groups", "dp"), "tensor"),
            P("tensor", None, None),
            P("tensor", None, None),
        ),
        out_specs=(
            P(("groups", "dp"), "tensor"),
            P(("groups", "tensor"), "dp", None),
            P(("groups", "tensor"), "dp", None),
        ),
        check_vma=False,
    )
```

```python
import math

import jax
import jax.numpy as jnp
from jax import lax
from jax.sharding import PartitionSpec as P

NB = 16
CHUNKS = 4


def expanded_weights(w_first, w_second, n_dev, order):
    blk_local, bs, _ = w_first.shape
    sub = bs // NB
    feat = blk_local * bs
    eye = jnp.eye(blk_local, dtype=jnp.bool_)
    zero = jnp.zeros((), w_first.dtype)
    w1r = jnp.take(w_first.reshape(blk_local, bs, n_dev, blk_local, sub), order, axis=2)
    w1p = jnp.where(
        eye[:, None, None, None, :, None], w1r[:, :, :, :, None, :], zero
    ).reshape(feat, feat)
    w2r = jnp.take(w_second.reshape(blk_local, sub, n_dev, blk_local, bs), order, axis=2)
    w2r = w2r.transpose(0, 4, 2, 3, 1)
    w2p = jnp.where(
        eye[:, None, None, :, None, None], w2r[:, :, :, None, :, :], zero
    ).reshape(feat, feat)
    w1t = w1r.transpose(2, 3, 4, 0, 1)
    w1tp = jnp.where(
        eye[None, None, :, None, :, None], w1t[:, :, None, :, :, :], zero
    ).reshape(feat, feat)
    return w1p, w2p, w1tp


def exchange(pieces, n_dev):
    outs = [pieces[0]]
    for m in range(1, n_dev):
        outs.append(lax.ppermute(pieces[m], "tensor", [(i, i ^ m) for i in range(n_dev)]))
    return outs


def dp_reduce_scatter(x):
    n = lax.axis_size("dp")
    didx = lax.axis_index("dp")
    blocks = x.reshape((n, x.shape[0] // n) + x.shape[1:])
    acc = lax.dynamic_index_in_dim(blocks, didx, axis=0, keepdims=False)
    for m in range(1, n):
        send = lax.dynamic_index_in_dim(blocks, jnp.bitwise_xor(didx, m), axis=0, keepdims=False)
        acc = acc + lax.ppermute(send, "dp", [(i, i ^ m) for i in range(n)])
    return acc


def second_gradient(gs_acc, order, n_dev, blk_local, sub, bs, grad_scale):
    eye = jnp.eye(blk_local, dtype=jnp.bool_)
    gs6 = gs_acc.reshape(n_dev, blk_local, blk_local, sub, blk_local, bs)
    gsd = jnp.sum(jnp.where(eye[None, :, None, None, :, None], gs6, 0.0), axis=4)
    gsd = jnp.take(gsd, order, axis=0)
    second_term = gsd.transpose(3, 0, 2, 1, 4).reshape(bs, blk_local, bs) * grad_scale
    return dp_reduce_scatter(second_term)


def shards(tokens, cotangent, w_first, w_second):
    tok_rows = tokens.shape[0]
    blk_local, bs, _ = w_first.shape
    feat = blk_local * bs
    sub = bs // NB
    part = feat // lax.axis_size("tensor")
    n_dev = lax.axis_size("tensor")
    dp_count = lax.axis_size("dp")
    grad_scale = 1.0 / math.sqrt(tok_rows * dp_count)
    idx = lax.axis_index("tensor")
    order = jnp.bitwise_xor(idx, jnp.arange(n_dev, dtype=idx.dtype))
    w1p, w2p, w1tp = expanded_weights(w_first, w_second, n_dev, order)
    step = tok_rows // CHUNKS

    eye = jnp.eye(blk_local, dtype=jnp.bool_)
    gf_acc = None
    gs_acc = None
    grad_tokens = jnp.zeros((tok_rows, feat), jnp.bfloat16)
    pending = []
    for k in range(CHUNKS):
        x = tokens[k * step:(k + 1) * step]
        cot = cotangent[k * step:(k + 1) * step]
        hidden = jnp.dot(x, w1p, preferred_element_type=jnp.float32).astype(jnp.bfloat16)
        backed = jnp.dot(cot, w2p, preferred_element_type=jnp.float32)
        moved = exchange([hidden[:, m * part:(m + 1) * part] for m in range(n_dev)], n_dev)
        masked = [
            jnp.where(moved[m] > 0, backed[:, m * part:(m + 1) * part], 0.0).astype(jnp.bfloat16)
            for m in range(n_dev)
        ]
        active = jnp.maximum(jnp.concatenate(moved, axis=1), jnp.zeros((), jnp.bfloat16))
        gs = lax.dot_general(
            active, cot, (((0,), (0,)), ((), ())), preferred_element_type=jnp.float32
        )
        gs_acc = gs if gs_acc is None else gs_acc + gs
        if len(pending) == 2:
            masked, done = lax.optimization_barrier((masked, pending.pop(0)))
            grad_tokens = lax.dynamic_update_slice(grad_tokens, done[0], (done[2], 0))
            gf_acc = done[1] if gf_acc is None else gf_acc + done[1]
        returned = jnp.concatenate(exchange(masked, n_dev), axis=1)
        if k + 1 == CHUNKS:
            grad_second = second_gradient(gs_acc, order, n_dev, blk_local, sub, bs, grad_scale)
            returned, grad_second = lax.optimization_barrier((returned, grad_second))
        gt = jnp.dot(returned, w1tp, preferred_element_type=jnp.float32).astype(jnp.bfloat16)
        gf = lax.dot_general(
            x, returned, (((0,), (0,)), ((), ())), preferred_element_type=jnp.float32
        )
        pending.append((gt, gf, k * step))
    for gt, gf, at in pending:
        grad_tokens = lax.dynamic_update_slice(grad_tokens, gt, (at, 0))
        gf_acc = gf if gf_acc is None else gf_acc + gf

    gf6 = gf_acc.reshape(blk_local, bs, n_dev, blk_local, blk_local, sub)
    gfd = jnp.sum(jnp.where(eye[:, None, None, None, :, None], gf6, 0.0), axis=4)
    gfd = jnp.take(gfd, order, axis=2)
    first_term = gfd.transpose(1, 0, 2, 3, 4).reshape(bs, blk_local, bs) * grad_scale
    grad_first = dp_reduce_scatter(first_term)
    return (grad_tokens, grad_first.transpose(1, 0, 2), grad_second.transpose(1, 0, 2))


def solution(mesh):
    return jax.shard_map(
        shards,
        mesh=mesh,
        in_specs=(
            P(("groups", "dp"), "tensor"),
            P(("groups", "dp"), "tensor"),
            P("tensor", None, None),
            P("tensor", None, None),
        ),
        out_specs=(
            P(("groups", "dp"), "tensor"),
            P(("groups", "tensor"), "dp", None),
            P(("groups", "tensor"), "dp", None),
        ),
        check_vma=False,
    )
```

```python
import math

import jax
import jax.numpy as jnp
from jax import lax
from jax.sharding import PartitionSpec as P

NB = 16
CHUNKS = 4


def expanded_weights(w_first, w_second, n_dev, order):
    blk_local, bs, _ = w_first.shape
    sub = bs // NB
    feat = blk_local * bs
    eye = jnp.eye(blk_local, dtype=jnp.bool_)
    zero = jnp.zeros((), w_first.dtype)
    w1r = jnp.take(w_first.reshape(blk_local, bs, n_dev, blk_local, sub), order, axis=2)
    w1p = jnp.where(
        eye[:, None, None, None, :, None], w1r[:, :, :, :, None, :], zero
    ).reshape(feat, feat)
    w2r = jnp.take(w_second.reshape(blk_local, sub, n_dev, blk_local, bs), order, axis=2)
    w2r = w2r.transpose(0, 4, 2, 3, 1)
    w2p = jnp.where(
        eye[:, None, None, :, None, None], w2r[:, :, :, None, :, :], zero
    ).reshape(feat, feat)
    w1t = w1r.transpose(2, 3, 4, 0, 1)
    w1tp = jnp.where(
        eye[None, None, :, None, :, None], w1t[:, :, None, :, :, :], zero
    ).reshape(feat, feat)
    return w1p, w2p, w1tp


def exchange(pieces, n_dev):
    outs = [pieces[0]]
    for m in range(1, n_dev):
        outs.append(lax.ppermute(pieces[m], "tensor", [(i, i ^ m) for i in range(n_dev)]))
    return outs


def dp_reduce_scatter(x):
    n = lax.axis_size("dp")
    didx = lax.axis_index("dp")
    blocks = x.reshape((n, x.shape[0] // n) + x.shape[1:])
    acc = lax.dynamic_index_in_dim(blocks, didx, axis=0, keepdims=False)
    for m in range(1, n):
        send = lax.dynamic_index_in_dim(blocks, jnp.bitwise_xor(didx, m), axis=0, keepdims=False)
        acc = acc + lax.ppermute(send, "dp", [(i, i ^ m) for i in range(n)])
    return acc


def shards(tokens, cotangent, w_first, w_second):
    tok_rows = tokens.shape[0]
    blk_local, bs, _ = w_first.shape
    feat = blk_local * bs
    sub = bs // NB
    part = feat // lax.axis_size("tensor")
    n_dev = lax.axis_size("tensor")
    dp_count = lax.axis_size("dp")
    grad_scale = 1.0 / math.sqrt(tok_rows * dp_count)
    idx = lax.axis_index("tensor")
    order = jnp.bitwise_xor(idx, jnp.arange(n_dev, dtype=idx.dtype))
    w1p, w2p, w1tp = expanded_weights(w_first, w_second, n_dev, order)
    step = tok_rows // CHUNKS

    eye = jnp.eye(blk_local, dtype=jnp.bool_)
    gf_acc = None
    gs_acc = None
    grad_tokens = jnp.zeros((tok_rows, feat), jnp.bfloat16)
    pending = []
    for k in range(CHUNKS):
        x = tokens[k * step:(k + 1) * step]
        cot = cotangent[k * step:(k + 1) * step]
        hidden = jnp.dot(x, w1p, preferred_element_type=jnp.float32).astype(jnp.bfloat16)
        backed = jnp.dot(cot, w2p, preferred_element_type=jnp.float32)
        moved = exchange([hidden[:, m * part:(m + 1) * part] for m in range(n_dev)], n_dev)
        masked = [
            jnp.where(moved[m] > 0, backed[:, m * part:(m + 1) * part], 0.0).astype(jnp.bfloat16)
            for m in range(n_dev)
        ]
        active = jnp.maximum(jnp.concatenate(moved, axis=1), jnp.zeros((), jnp.bfloat16))
        gs = lax.dot_general(
            active, cot, (((0,), (0,)), ((), ())), preferred_element_type=jnp.float32
        )
        gs_acc = gs if gs_acc is None else gs_acc + gs
        if len(pending) == 2:
            masked, done = lax.optimization_barrier((masked, pending.pop(0)))
            grad_tokens = lax.dynamic_update_slice(grad_tokens, done[0], (done[2], 0))
            gf_acc = done[1] if gf_acc is None else gf_acc + done[1]
        returned = jnp.concatenate(exchange(masked, n_dev), axis=1)
        gt = jnp.dot(returned, w1tp, preferred_element_type=jnp.float32).astype(jnp.bfloat16)
        gf = lax.dot_general(
            x, returned, (((0,), (0,)), ((), ())), preferred_element_type=jnp.float32
        )
        pending.append((gt, gf, k * step))
    gf_last = None
    for gt, gf, at in pending:
        grad_tokens = lax.dynamic_update_slice(grad_tokens, gt, (at, 0))
        if at == (CHUNKS - 1) * step:
            gf_last = gf
        else:
            gf_acc = gf if gf_acc is None else gf_acc + gf

    gs6 = gs_acc.reshape(n_dev, blk_local, blk_local, sub, blk_local, bs)
    gsd = jnp.sum(jnp.where(eye[None, :, None, None, :, None], gs6, 0.0), axis=4)
    gsd = jnp.take(gsd, order, axis=0)
    second_term = gsd.transpose(3, 0, 2, 1, 4).reshape(bs, blk_local, bs) * grad_scale
    grad_second = lax.psum_scatter(second_term, "dp", scatter_dimension=0, tiled=True)
    gf_acc, grad_second = lax.optimization_barrier((gf_acc, grad_second))
    def diagonal_blocks(g):
        g6 = g.reshape(blk_local, bs, n_dev, blk_local, blk_local, sub)
        return jnp.sum(jnp.where(eye[:, None, None, None, :, None], g6, 0.0), axis=4)

    gfd = diagonal_blocks(gf_acc) + diagonal_blocks(gf_last)
    gfd = jnp.take(gfd, order, axis=2)
    first_term = gfd.transpose(1, 0, 2, 3, 4).reshape(bs, blk_local, bs) * grad_scale
    grad_first = dp_reduce_scatter(first_term)
    return (grad_tokens, grad_first.transpose(1, 0, 2), grad_second.transpose(1, 0, 2))


def solution(mesh):
    return jax.shard_map(
        shards,
        mesh=mesh,
        in_specs=(
            P(("groups", "dp"), "tensor"),
            P(("groups", "dp"), "tensor"),
            P("tensor", None, None),
            P("tensor", None, None),
        ),
        out_specs=(
            P(("groups", "dp"), "tensor"),
            P(("groups", "tensor"), "dp", None),
            P(("groups", "tensor"), "dp", None),
        ),
        check_vma=False,
    )
```

```python
import math

import jax
import jax.numpy as jnp
from jax import lax
from jax.sharding import PartitionSpec as P

NB = 16
CHUNKS = 4


def expanded_weights(w_first, w_second, n_dev, order):
    blk_local, bs, _ = w_first.shape
    sub = bs // NB
    feat = blk_local * bs
    eye = jnp.eye(blk_local, dtype=jnp.bool_)
    zero = jnp.zeros((), w_first.dtype)
    w1r = jnp.take(w_first.reshape(blk_local, bs, n_dev, blk_local, sub), order, axis=2)
    w1p = jnp.where(
        eye[:, None, None, None, :, None], w1r[:, :, :, :, None, :], zero
    ).reshape(feat, feat)
    w2r = jnp.take(w_second.reshape(blk_local, sub, n_dev, blk_local, bs), order, axis=2)
    w2r = w2r.transpose(0, 4, 2, 3, 1)
    w2p = jnp.where(
        eye[:, None, None, :, None, None], w2r[:, :, :, None, :, :], zero
    ).reshape(feat, feat)
    w1t = w1r.transpose(2, 3, 4, 0, 1)
    w1tp = jnp.where(
        eye[None, None, :, None, :, None], w1t[:, :, None, :, :, :], zero
    ).reshape(feat, feat)
    return w1p, w2p, w1tp


def exchange(pieces, n_dev):
    outs = [pieces[0]]
    for m in range(1, n_dev):
        outs.append(lax.ppermute(pieces[m], "tensor", [(i, i ^ m) for i in range(n_dev)]))
    return outs


def dp_reduce_scatter(x):
    n = lax.axis_size("dp")
    didx = lax.axis_index("dp")
    blocks = x.reshape((n, x.shape[0] // n) + x.shape[1:])
    acc = lax.dynamic_index_in_dim(blocks, didx, axis=0, keepdims=False)
    for m in range(1, n):
        send = lax.dynamic_index_in_dim(blocks, jnp.bitwise_xor(didx, m), axis=0, keepdims=False)
        acc = acc + lax.ppermute(send, "dp", [(i, i ^ m) for i in range(n)])
    return acc


def shards(tokens, cotangent, w_first, w_second):
    tok_rows = tokens.shape[0]
    blk_local, bs, _ = w_first.shape
    feat = blk_local * bs
    sub = bs // NB
    part = feat // lax.axis_size("tensor")
    n_dev = lax.axis_size("tensor")
    dp_count = lax.axis_size("dp")
    grad_scale = 1.0 / math.sqrt(tok_rows * dp_count)
    idx = lax.axis_index("tensor")
    order = jnp.bitwise_xor(idx, jnp.arange(n_dev, dtype=idx.dtype))
    w1p, w2p, w1tp = expanded_weights(w_first, w_second, n_dev, order)
    step = tok_rows // CHUNKS

    eye = jnp.eye(blk_local, dtype=jnp.bool_)
    gf_acc = None
    gs_acc = None
    grad_tokens = jnp.zeros((tok_rows, feat), jnp.bfloat16)
    pending = []
    for k in range(CHUNKS):
        x = tokens[k * step:(k + 1) * step]
        cot = cotangent[k * step:(k + 1) * step]
        hidden = jnp.dot(x, w1p, preferred_element_type=jnp.float32).astype(jnp.bfloat16)
        backed = jnp.dot(cot, w2p, preferred_element_type=jnp.float32)
        moved = exchange([hidden[:, m * part:(m + 1) * part] for m in range(n_dev)], n_dev)
        masked = [
            jnp.where(moved[m] > 0, backed[:, m * part:(m + 1) * part], 0.0).astype(jnp.bfloat16)
            for m in range(n_dev)
        ]
        active = jnp.maximum(jnp.concatenate(moved, axis=1), jnp.zeros((), jnp.bfloat16))
        gs = lax.dot_general(
            active, cot, (((0,), (0,)), ((), ())), preferred_element_type=jnp.float32
        )
        gs_acc = gs if gs_acc is None else gs_acc + gs
        if len(pending) == 2:
            masked, done = lax.optimization_barrier((masked, pending.pop(0)))
            grad_tokens = lax.dynamic_update_slice(grad_tokens, done[0], (done[2], 0))
            gf_acc = done[1] if gf_acc is None else gf_acc + done[1]
        returned = jnp.concatenate(exchange(masked, n_dev), axis=1)
        gt = jnp.dot(returned, w1tp, preferred_element_type=jnp.float32).astype(jnp.bfloat16)
        if k + 1 < CHUNKS:
            gf = lax.dot_general(
                x, returned, (((0,), (0,)), ((), ())), preferred_element_type=jnp.float32
            )
        else:
            gf = jnp.einsum(
                "tmcbq,tbi->bimcq",
                returned.reshape(step, n_dev, blk_local, blk_local, sub),
                x.reshape(step, blk_local, bs),
                preferred_element_type=jnp.float32,
            )
        pending.append((gt, gf, k * step))
    gf_last = None
    for gt, gf, at in pending:
        grad_tokens = lax.dynamic_update_slice(grad_tokens, gt, (at, 0))
        if at == (CHUNKS - 1) * step:
            gf_last = gf
        else:
            gf_acc = gf if gf_acc is None else gf_acc + gf

    gs6 = gs_acc.reshape(n_dev, blk_local, blk_local, sub, blk_local, bs)
    gsd = jnp.sum(jnp.where(eye[None, :, None, None, :, None], gs6, 0.0), axis=4)
    gsd = jnp.take(gsd, order, axis=0)
    second_term = gsd.transpose(3, 0, 2, 1, 4).reshape(bs, blk_local, bs) * grad_scale
    grad_second = lax.psum_scatter(second_term, "dp", scatter_dimension=0, tiled=True)
    gf_acc, grad_second = lax.optimization_barrier((gf_acc, grad_second))
    def diagonal_blocks(g):
        g6 = g.reshape(blk_local, bs, n_dev, blk_local, blk_local, sub)
        return jnp.sum(jnp.where(eye[:, None, None, None, :, None], g6, 0.0), axis=4)

    gfd = diagonal_blocks(gf_acc) + gf_last
    gfd = jnp.take(gfd, order, axis=2)
    first_term = gfd.transpose(1, 0, 2, 3, 4).reshape(bs, blk_local, bs) * grad_scale
    grad_first = dp_reduce_scatter(first_term)
    return (grad_tokens, grad_first.transpose(1, 0, 2), grad_second.transpose(1, 0, 2))


def solution(mesh):
    return jax.shard_map(
        shards,
        mesh=mesh,
        in_specs=(
            P(("groups", "dp"), "tensor"),
            P(("groups", "dp"), "tensor"),
            P("tensor", None, None),
            P("tensor", None, None),
        ),
        out_specs=(
            P(("groups", "dp"), "tensor"),
            P(("groups", "tensor"), "dp", None),
            P(("groups", "tensor"), "dp", None),
        ),
        check_vma=False,
    )
```

```python
import math

import jax
import jax.numpy as jnp
from jax import lax
from jax.sharding import PartitionSpec as P

NB = 16
CHUNKS = 4


def expanded_weights(w_first, w_second, n_dev, order):
    blk_local, bs, _ = w_first.shape
    sub = bs // NB
    feat = blk_local * bs
    eye = jnp.eye(blk_local, dtype=jnp.bool_)
    zero = jnp.zeros((), w_first.dtype)
    w1r = jnp.take(w_first.reshape(blk_local, bs, n_dev, blk_local, sub), order, axis=2)
    w1p = jnp.where(
        eye[:, None, None, None, :, None], w1r[:, :, :, :, None, :], zero
    ).reshape(feat, feat)
    w2r = jnp.take(w_second.reshape(blk_local, sub, n_dev, blk_local, bs), order, axis=2)
    w2r = w2r.transpose(0, 4, 2, 3, 1)
    w2p = jnp.where(
        eye[:, None, None, :, None, None], w2r[:, :, :, None, :, :], zero
    ).reshape(feat, feat)
    w1t = w1r.transpose(2, 3, 4, 0, 1)
    w1tp = jnp.where(
        eye[None, None, :, None, :, None], w1t[:, :, None, :, :, :], zero
    ).reshape(feat, feat)
    return w1p, w2p, w1tp


def exchange(pieces, n_dev):
    outs = [pieces[0]]
    for m in range(1, n_dev):
        outs.append(lax.ppermute(pieces[m], "tensor", [(i, i ^ m) for i in range(n_dev)]))
    return outs


def dp_reduce_scatter(x):
    n = lax.axis_size("dp")
    didx = lax.axis_index("dp")
    blocks = x.reshape((n, x.shape[0] // n) + x.shape[1:])
    acc = lax.dynamic_index_in_dim(blocks, didx, axis=0, keepdims=False)
    for m in range(1, n):
        send = lax.dynamic_index_in_dim(blocks, jnp.bitwise_xor(didx, m), axis=0, keepdims=False)
        acc = acc + lax.ppermute(send, "dp", [(i, i ^ m) for i in range(n)])
    return acc


def shards(tokens, cotangent, w_first, w_second):
    tok_rows = tokens.shape[0]
    blk_local, bs, _ = w_first.shape
    feat = blk_local * bs
    sub = bs // NB
    part = feat // lax.axis_size("tensor")
    n_dev = lax.axis_size("tensor")
    dp_count = lax.axis_size("dp")
    grad_scale = 1.0 / math.sqrt(tok_rows * dp_count)
    idx = lax.axis_index("tensor")
    order = jnp.bitwise_xor(idx, jnp.arange(n_dev, dtype=idx.dtype))
    w1p, w2p, w1tp = expanded_weights(w_first, w_second, n_dev, order)
    step = tok_rows // CHUNKS

    eye = jnp.eye(blk_local, dtype=jnp.bool_)
    gf_acc = None
    gs_acc = None
    grad_tokens = jnp.zeros((tok_rows, feat), jnp.bfloat16)
    pending = []
    for k in range(CHUNKS):
        x = tokens[k * step:(k + 1) * step]
        cot = cotangent[k * step:(k + 1) * step]
        hidden = jnp.dot(x, w1p, preferred_element_type=jnp.float32).astype(jnp.bfloat16)
        backed = jnp.dot(cot, w2p, preferred_element_type=jnp.float32)
        moved = exchange([hidden[:, m * part:(m + 1) * part] for m in range(n_dev)], n_dev)
        masked = [
            jnp.where(moved[m] > 0, backed[:, m * part:(m + 1) * part], 0.0).astype(jnp.bfloat16)
            for m in range(n_dev)
        ]
        active = jnp.maximum(jnp.concatenate(moved, axis=1), jnp.zeros((), jnp.bfloat16))
        gs = lax.dot_general(
            active, cot, (((0,), (0,)), ((), ())), preferred_element_type=jnp.float32
        )
        gs_acc = gs if gs_acc is None else gs_acc + gs
        if len(pending) == 2:
            masked, done = lax.optimization_barrier((masked, pending.pop(0)))
            grad_tokens = lax.dynamic_update_slice(grad_tokens, done[0], (done[2], 0))
            gf_acc = done[1] if gf_acc is None else gf_acc + done[1]
        returned = jnp.concatenate(exchange(masked, n_dev), axis=1)
        gt = jnp.dot(returned, w1tp, preferred_element_type=jnp.float32).astype(jnp.bfloat16)
        if k + 2 < CHUNKS:
            gf = lax.dot_general(
                x, returned, (((0,), (0,)), ((), ())), preferred_element_type=jnp.float32
            )
        else:
            gf = jnp.einsum(
                "tmcbq,tbi->bimcq",
                returned.reshape(step, n_dev, blk_local, blk_local, sub),
                x.reshape(step, blk_local, bs),
                preferred_element_type=jnp.float32,
            )
        pending.append((gt, gf, k * step))
    gf_last = None
    for gt, gf, at in pending:
        grad_tokens = lax.dynamic_update_slice(grad_tokens, gt, (at, 0))
        if at >= (CHUNKS - 2) * step:
            gf_last = gf if gf_last is None else gf_last + gf
        else:
            gf_acc = gf if gf_acc is None else gf_acc + gf

    gs6 = gs_acc.reshape(n_dev, blk_local, blk_local, sub, blk_local, bs)
    gsd = jnp.sum(jnp.where(eye[None, :, None, None, :, None], gs6, 0.0), axis=4)
    gsd = jnp.take(gsd, order, axis=0)
    second_term = gsd.transpose(3, 0, 2, 1, 4).reshape(bs, blk_local, bs) * grad_scale
    grad_second = lax.psum_scatter(second_term, "dp", scatter_dimension=0, tiled=True)
    gf_acc, grad_second = lax.optimization_barrier((gf_acc, grad_second))
    def diagonal_blocks(g):
        g6 = g.reshape(blk_local, bs, n_dev, blk_local, blk_local, sub)
        return jnp.sum(jnp.where(eye[:, None, None, None, :, None], g6, 0.0), axis=4)

    gfd = diagonal_blocks(gf_acc) + gf_last
    gfd = jnp.take(gfd, order, axis=2)
    first_term = gfd.transpose(1, 0, 2, 3, 4).reshape(bs, blk_local, bs) * grad_scale
    grad_first = dp_reduce_scatter(first_term)
    return (grad_tokens, grad_first.transpose(1, 0, 2), grad_second.transpose(1, 0, 2))


def solution(mesh):
    return jax.shard_map(
        shards,
        mesh=mesh,
        in_specs=(
            P(("groups", "dp"), "tensor"),
            P(("groups", "dp"), "tensor"),
            P("tensor", None, None),
            P("tensor", None, None),
        ),
        out_specs=(
            P(("groups", "dp"), "tensor"),
            P(("groups", "tensor"), "dp", None),
            P(("groups", "tensor"), "dp", None),
        ),
        check_vma=False,
    )
```

```python
import math

import jax
import jax.numpy as jnp
from jax import lax
from jax.sharding import PartitionSpec as P

NB = 16
CHUNKS = 4


def expanded_weights(w_first, w_second, n_dev, order):
    blk_local, bs, _ = w_first.shape
    sub = bs // NB
    feat = blk_local * bs
    eye = jnp.eye(blk_local, dtype=jnp.bool_)
    zero = jnp.zeros((), w_first.dtype)
    w1r = jnp.take(w_first.reshape(blk_local, bs, n_dev, blk_local, sub), order, axis=2)
    w1p = jnp.where(
        eye[:, None, None, None, :, None], w1r[:, :, :, :, None, :], zero
    ).reshape(feat, feat)
    w2r = jnp.take(w_second.reshape(blk_local, sub, n_dev, blk_local, bs), order, axis=2)
    w2r = w2r.transpose(0, 4, 2, 3, 1)
    w2p = jnp.where(
        eye[:, None, None, :, None, None], w2r[:, :, :, None, :, :], zero
    ).reshape(feat, feat)
    w1t = w1r.transpose(2, 3, 4, 0, 1)
    w1tp = jnp.where(
        eye[None, None, :, None, :, None], w1t[:, :, None, :, :, :], zero
    ).reshape(feat, feat)
    return w1p, w2p, w1tp


def exchange(pieces, n_dev):
    outs = [pieces[0]]
    for m in range(1, n_dev):
        outs.append(lax.ppermute(pieces[m], "tensor", [(i, i ^ m) for i in range(n_dev)]))
    return outs


def dp_reduce_scatter(x):
    n = lax.axis_size("dp")
    didx = lax.axis_index("dp")
    blocks = x.reshape((n, x.shape[0] // n) + x.shape[1:])
    acc = lax.dynamic_index_in_dim(blocks, didx, axis=0, keepdims=False)
    for m in range(1, n):
        send = lax.dynamic_index_in_dim(blocks, jnp.bitwise_xor(didx, m), axis=0, keepdims=False)
        acc = acc + lax.ppermute(send, "dp", [(i, i ^ m) for i in range(n)])
    return acc


def shards(tokens, cotangent, w_first, w_second):
    tok_rows = tokens.shape[0]
    blk_local, bs, _ = w_first.shape
    feat = blk_local * bs
    sub = bs // NB
    part = feat // lax.axis_size("tensor")
    n_dev = lax.axis_size("tensor")
    dp_count = lax.axis_size("dp")
    grad_scale = 1.0 / math.sqrt(tok_rows * dp_count)
    idx = lax.axis_index("tensor")
    order = jnp.bitwise_xor(idx, jnp.arange(n_dev, dtype=idx.dtype))
    w1p, w2p, w1tp = expanded_weights(w_first, w_second, n_dev, order)
    step = tok_rows // CHUNKS

    eye = jnp.eye(blk_local, dtype=jnp.bool_)
    gf_acc = None
    gs_acc = None
    grad_tokens = jnp.zeros((tok_rows, feat), jnp.bfloat16)
    pending = []
    for k in range(CHUNKS):
        x = tokens[k * step:(k + 1) * step]
        cot = cotangent[k * step:(k + 1) * step]
        hidden = jnp.dot(x, w1p, preferred_element_type=jnp.float32).astype(jnp.bfloat16)
        backed = jnp.dot(cot, w2p, preferred_element_type=jnp.float32)
        moved = exchange([hidden[:, m * part:(m + 1) * part] for m in range(n_dev)], n_dev)
        masked = [
            jnp.where(moved[m] > 0, backed[:, m * part:(m + 1) * part], 0.0).astype(jnp.bfloat16)
            for m in range(n_dev)
        ]
        active = jnp.maximum(jnp.concatenate(moved, axis=1), jnp.zeros((), jnp.bfloat16))
        gs = lax.dot_general(
            active, cot, (((0,), (0,)), ((), ())), preferred_element_type=jnp.float32
        )
        gs_acc = gs if gs_acc is None else gs_acc + gs
        if len(pending) == 2:
            masked, done = lax.optimization_barrier((masked, pending.pop(0)))
            grad_tokens = lax.dynamic_update_slice(grad_tokens, done[0], (done[2], 0))
            gf_acc = done[1] if gf_acc is None else gf_acc + done[1]
        returned = jnp.concatenate(exchange(masked, n_dev), axis=1)
        gt = jnp.dot(returned, w1tp, preferred_element_type=jnp.float32).astype(jnp.bfloat16)
        if k + 1 < CHUNKS:
            gf = lax.dot_general(
                x, returned, (((0,), (0,)), ((), ())), preferred_element_type=jnp.float32
            )
        else:
            gf = jnp.einsum(
                "tmcbq,tbi->bimcq",
                returned.reshape(step, n_dev, blk_local, blk_local, sub),
                x.reshape(step, blk_local, bs),
                preferred_element_type=jnp.float32,
            )
        pending.append((gt, gf, k * step))
    gf_last = None
    gf_mid = []
    for gt, gf, at in pending:
        grad_tokens = lax.dynamic_update_slice(grad_tokens, gt, (at, 0))
        if at == (CHUNKS - 1) * step:
            gf_last = gf
        else:
            gf_mid.append(gf)

    gs6 = gs_acc.reshape(n_dev, blk_local, blk_local, sub, blk_local, bs)
    gsd = jnp.sum(jnp.where(eye[None, :, None, None, :, None], gs6, 0.0), axis=4)
    gsd = jnp.take(gsd, order, axis=0)
    second_term = gsd.transpose(3, 0, 2, 1, 4).reshape(bs, blk_local, bs) * grad_scale
    grad_second = lax.psum_scatter(second_term, "dp", scatter_dimension=0, tiled=True)
    gf_acc, grad_second = lax.optimization_barrier((gf_acc, grad_second))
    def diagonal_blocks(g):
        g6 = g.reshape(blk_local, bs, n_dev, blk_local, blk_local, sub)
        return jnp.sum(jnp.where(eye[:, None, None, None, :, None], g6, 0.0), axis=4)

    gfd = diagonal_blocks(gf_acc)
    for gf in gf_mid:
        gfd = gfd + diagonal_blocks(gf)
    gfd = gfd + gf_last
    gfd = jnp.take(gfd, order, axis=2)
    first_term = gfd.transpose(1, 0, 2, 3, 4).reshape(bs, blk_local, bs) * grad_scale
    grad_first = dp_reduce_scatter(first_term)
    return (grad_tokens, grad_first.transpose(1, 0, 2), grad_second.transpose(1, 0, 2))


def solution(mesh):
    return jax.shard_map(
        shards,
        mesh=mesh,
        in_specs=(
            P(("groups", "dp"), "tensor"),
            P(("groups", "dp"), "tensor"),
            P("tensor", None, None),
            P("tensor", None, None),
        ),
        out_specs=(
            P(("groups", "dp"), "tensor"),
            P(("groups", "tensor"), "dp", None),
            P(("groups", "tensor"), "dp", None),
        ),
        check_vma=False,
    )
```

```python
import math

import jax
import jax.numpy as jnp
from jax import lax
from jax.sharding import PartitionSpec as P

NB = 16
CHUNKS = 4


def expanded_weights(w_first, w_second, n_dev, order):
    blk_local, bs, _ = w_first.shape
    sub = bs // NB
    feat = blk_local * bs
    eye = jnp.eye(blk_local, dtype=jnp.bool_)
    zero = jnp.zeros((), w_first.dtype)
    w1r = jnp.take(w_first.reshape(blk_local, bs, n_dev, blk_local, sub), order, axis=2)
    w1p = jnp.where(
        eye[:, None, None, None, :, None], w1r[:, :, :, :, None, :], zero
    ).reshape(feat, feat)
    w2r = jnp.take(w_second.reshape(blk_local, sub, n_dev, blk_local, bs), order, axis=2)
    w2r = w2r.transpose(0, 4, 2, 3, 1)
    w2p = jnp.where(
        eye[:, None, None, :, None, None], w2r[:, :, :, None, :, :], zero
    ).reshape(feat, feat)
    w1t = w1r.transpose(2, 3, 4, 0, 1)
    w1tp = jnp.where(
        eye[None, None, :, None, :, None], w1t[:, :, None, :, :, :], zero
    ).reshape(feat, feat)
    return w1p, w2p, w1tp


def exchange(pieces, n_dev):
    outs = [pieces[0]]
    for m in range(1, n_dev):
        outs.append(lax.ppermute(pieces[m], "tensor", [(i, i ^ m) for i in range(n_dev)]))
    return outs


def dp_reduce_scatter(x):
    n = lax.axis_size("dp")
    didx = lax.axis_index("dp")
    blocks = x.reshape((n, x.shape[0] // n) + x.shape[1:])
    acc = lax.dynamic_index_in_dim(blocks, didx, axis=0, keepdims=False)
    for m in range(1, n):
        send = lax.dynamic_index_in_dim(blocks, jnp.bitwise_xor(didx, m), axis=0, keepdims=False)
        acc = acc + lax.ppermute(send, "dp", [(i, i ^ m) for i in range(n)])
    return acc


def shards(tokens, cotangent, w_first, w_second):
    tok_rows = tokens.shape[0]
    blk_local, bs, _ = w_first.shape
    feat = blk_local * bs
    sub = bs // NB
    part = feat // lax.axis_size("tensor")
    n_dev = lax.axis_size("tensor")
    dp_count = lax.axis_size("dp")
    grad_scale = 1.0 / math.sqrt(tok_rows * dp_count)
    idx = lax.axis_index("tensor")
    order = jnp.bitwise_xor(idx, jnp.arange(n_dev, dtype=idx.dtype))
    w1p, w2p, w1tp = expanded_weights(w_first, w_second, n_dev, order)
    step = tok_rows // CHUNKS

    eye = jnp.eye(blk_local, dtype=jnp.bool_)
    gf_acc = None
    gs_acc = None
    grad_tokens = jnp.zeros((tok_rows, feat), jnp.bfloat16)
    pending = []
    for k in range(CHUNKS):
        x = tokens[k * step:(k + 1) * step]
        cot = cotangent[k * step:(k + 1) * step]
        hidden = jnp.dot(x, w1p, preferred_element_type=jnp.float32).astype(jnp.bfloat16)
        backed = jnp.dot(cot, w2p, preferred_element_type=jnp.float32)
        moved = exchange([hidden[:, m * part:(m + 1) * part] for m in range(n_dev)], n_dev)
        masked = [
            jnp.where(moved[m] > 0, backed[:, m * part:(m + 1) * part], 0.0).astype(jnp.bfloat16)
            for m in range(n_dev)
        ]
        active = jnp.maximum(jnp.concatenate(moved, axis=1), jnp.zeros((), jnp.bfloat16))
        gs = lax.dot_general(
            active, cot, (((0,), (0,)), ((), ())), preferred_element_type=jnp.float32
        )
        gs_acc = gs if gs_acc is None else gs_acc + gs
        if len(pending) == 2:
            masked, done = lax.optimization_barrier((masked, pending.pop(0)))
            grad_tokens = lax.dynamic_update_slice(grad_tokens, done[0], (done[2], 0))
            gf_acc = done[1] if gf_acc is None else gf_acc + done[1]
        returned = jnp.concatenate(exchange(masked, n_dev), axis=1)
        gt = jnp.dot(returned, w1tp, preferred_element_type=jnp.float32).astype(jnp.bfloat16)
        if k + 1 < CHUNKS:
            gf = lax.dot_general(
                x, returned, (((0,), (0,)), ((), ())), preferred_element_type=jnp.float32
            )
        else:
            gf = jnp.einsum(
                "tmcbq,tbi->bimcq",
                returned.reshape(step, n_dev, blk_local, blk_local, sub),
                x.reshape(step, blk_local, bs),
                preferred_element_type=jnp.float32,
            )
        pending.append((gt, gf, k * step))
    gf_last = None
    for gt, gf, at in pending:
        grad_tokens = lax.dynamic_update_slice(grad_tokens, gt, (at, 0))
        if at == (CHUNKS - 1) * step:
            gf_last = gf
        else:
            gf_acc = gf if gf_acc is None else gf_acc + gf

    gs6 = gs_acc.reshape(n_dev, blk_local, blk_local, sub, blk_local, bs)
    gsd = jnp.sum(jnp.where(eye[None, :, None, None, :, None], gs6, 0.0), axis=4)
    gsd = jnp.take(gsd, order, axis=0)
    second_term = gsd.transpose(3, 0, 2, 1, 4).reshape(bs, blk_local, bs) * grad_scale
    grad_second = lax.psum_scatter(second_term, "dp", scatter_dimension=0, tiled=True)
    def diagonal_blocks(g):
        g6 = g.reshape(blk_local, bs, n_dev, blk_local, blk_local, sub)
        return jnp.sum(jnp.where(eye[:, None, None, None, :, None], g6, 0.0), axis=4)

    gfd = diagonal_blocks(gf_acc) + gf_last
    gfd = jnp.take(gfd, order, axis=2)
    first_term = gfd.transpose(1, 0, 2, 3, 4).reshape(bs, blk_local, bs) * grad_scale
    grad_first = dp_reduce_scatter(first_term)
    return (grad_tokens, grad_first.transpose(1, 0, 2), grad_second.transpose(1, 0, 2))


def solution(mesh):
    return jax.shard_map(
        shards,
        mesh=mesh,
        in_specs=(
            P(("groups", "dp"), "tensor"),
            P(("groups", "dp"), "tensor"),
            P("tensor", None, None),
            P("tensor", None, None),
        ),
        out_specs=(
            P(("groups", "dp"), "tensor"),
            P(("groups", "tensor"), "dp", None),
            P(("groups", "tensor"), "dp", None),
        ),
        check_vma=False,
    )
```
